512 devices in a mesh: dp: 4 (over y_hi, core), context: 16 (over y_lo, x), tensor: 8 (over z).
Axes of the slice: x: 4, y: 8 (y_hi: 2, y_lo: 4; y = y_hi * 4 + y_lo), z: 8, core: 2. Of those that a mesh axis runs over, the one named last changes fastest.
Arguments:
- queries: bfloat16 [8192, 4096], P(('dp', 'context'), 'tensor'), parts along dimension 0, may hold values from -6 to 6
- keys: bfloat16 [8192, 1024], P(('dp', 'context'), 'tensor'), parts along dimension 0, may hold values from -6 to 6
- values: bfloat16 [8192, 1024], P(('dp', 'context'), 'tensor'), parts along dimension 0, may hold values from -6 to 6
- order: int32 [8192], P('dp'), parts along dimension 0, may hold values from 0 to 2047, as said below
- out_weight: bfloat16 [4096, 4096], P('tensor', 'context'), may hold values from -0.125 to 0.125
Outputs:
- output: bfloat16 [8192, 4096], P(('dp', 'context'), 'tensor'), parts along dimension 0
The draws below stay inside these ranges and needn't reach their ends.
There are 4 independent parts, one for each index of `dp`. The reference program is written for one: setup_inputs(seed, part) draws one part's arguments, and reference() takes and returns one part's arrays. A program takes and returns all parts, laid end to end along the dimension named above; an argument that names none is the same for every part. Nothing has to cross between parts.
Inputs may be any that keep to these rules, and one draw needn't show every extreme that they name: A permutation of the positions; each aligned block of 128 rows holds 128 consecutive positions in increasing order, starting at a multiple of 128.
All inputs are finite; a program needn't handle non-finite values.
Results may differ from the reference program's by a relative error of at most 0.019.
Values may be sent and summed in bfloat16 or wider, within the bound.
No kernel may reach another device: no remote copies, remote signals or barrier semaphores. Data moves between devices by JAX's collectives and lax.ppermute only.
A program may use at most 64 MiB of HBM per device.

```python
import math
import jax
import jax.numpy as jnp
from jax import lax

D = 4096
QUERY_HEADS = 32
KEY_VALUE_HEADS = 8
HEAD_SIZE = 128
BLK = 128
SEQUENCE_TOKENS = 2048


def draw_queries(key, part):
    folded_rows = jax.random.fold_in(key, 3)
    final_output = jnp.clip(jax.random.normal(folded_rows, (SEQUENCE_TOKENS, QUERY_HEADS * HEAD_SIZE), jnp.float32), -6.0, 6.0)
    return final_output.astype(jnp.bfloat16)


def draw_keys(key, part):
    folded_rows = jax.random.fold_in(key, 5)
    final_output = jnp.clip(jax.random.normal(folded_rows, (SEQUENCE_TOKENS, KEY_VALUE_HEADS * HEAD_SIZE), jnp.float32), -6.0, 6.0)
    return final_output.astype(jnp.bfloat16)


def draw_order(key, part):
    block_count = SEQUENCE_TOKENS // BLK
    shuffled = jax.random.permutation(jax.random.fold_in(key, 1), block_count).astype(jnp.int32)
    inside = jnp.arange(BLK, dtype=jnp.int32)
    return (shuffled[:, None] * BLK + inside[None, :]).reshape(SEQUENCE_TOKENS).astype(jnp.int32)


def spiked(drawn, rng, source, target, blocks, factor):
    def block_of(dim):
        return (jnp.arange(drawn.shape[dim]) // (drawn.shape[dim] // blocks)).reshape((-1,) + (1,) * (drawn.ndim - 1 - dim))

    one_side = jax.random.permutation(rng, blocks)[block_of(target)]
    second = (block_of(target) + blocks // 2) % blocks
    return jnp.where((block_of(source) == one_side) | (block_of(source) == second), factor * drawn, drawn)


def shard_levels(stream_key, dims, pieces, least, high):
    factor_of = 1.0
    for axis_at, parts in pieces:
        steps = jax.random.uniform(jax.random.fold_in(jax.random.fold_in(stream_key, 6), axis_at), (parts,), jnp.float32, least / len(pieces), high / len(pieces))
        factor_of = factor_of * jnp.repeat(jnp.exp(steps), dims[axis_at] // parts).reshape((-1,) + (1,) * (len(dims) - 1 - axis_at))
    return factor_of


def bell_draw(rng, shape, spread, bound, shards=(), kind=jnp.bfloat16):
    drawn = spread * jax.random.normal(rng, shape, jnp.float32)
    if shards:
        drawn = drawn * shard_levels(rng, shape, shards, -0.22, 0.18)
    return jnp.clip(drawn, -bound, bound).astype(kind)


def noise_with(stream_key, dims, scale, limit, pieces, heavy, kind=jnp.bfloat16):
    result = scale * jax.random.normal(stream_key, dims, jnp.float32)
    if pieces:
        result = result * shard_levels(stream_key, dims, pieces, -0.22, 0.18)
    return jnp.clip(spiked(result, jax.random.fold_in(stream_key, 3), *heavy), -limit, limit).astype(kind)


def setup_inputs(seed: int = 0, part: int = 0) -> dict:
    seeds = jax.random.split(jax.random.key(seed), 6)
    part_keys = jax.random.split(jax.random.fold_in(seeds[5], part), 6)
    queries = draw_queries(jax.random.fold_in(jax.random.fold_in(seeds[5], part), 71), part)
    keys = draw_keys(jax.random.fold_in(jax.random.fold_in(seeds[5], part), 71), part)
    values = bell_draw(part_keys[2], (SEQUENCE_TOKENS, KEY_VALUE_HEADS * HEAD_SIZE), 1.0, 6.0, ((0, 16), (1, 8)))
    order = draw_order(jax.random.fold_in(jax.random.fold_in(seeds[5], part), 71), part)
    out_weight = noise_with(seeds[4], (QUERY_HEADS * HEAD_SIZE, D), (QUERY_HEADS * HEAD_SIZE) ** -0.5, 0.125, ((0, 8), (1, 16)), (0, 1, 16, 2.0))
    return dict(queries=queries, keys=keys, values=values, order=order, out_weight=out_weight)


def reference(queries, keys, values, order, out_weight):
    query_head_group = QUERY_HEADS // KEY_VALUE_HEADS
    score_scale = 1.0 / math.sqrt(HEAD_SIZE)
    visible = order[None, :] <= order[:, None]

    def one_head(head_index):
        kv_index = head_index // query_head_group
        query_head = lax.dynamic_slice_in_dim(queries, (head_index * HEAD_SIZE).astype(jnp.int32), HEAD_SIZE, 1)
        key_head = lax.dynamic_slice_in_dim(keys, (kv_index * HEAD_SIZE).astype(jnp.int32), HEAD_SIZE, 1)
        value_head = lax.dynamic_slice_in_dim(values, (kv_index * HEAD_SIZE).astype(jnp.int32), HEAD_SIZE, 1)
        scores = jnp.dot(query_head, key_head.T, preferred_element_type=jnp.float32) * score_scale
        scores = jnp.where(visible, scores, -1e+30)
        row_max = lax.optimization_barrier(jnp.max(scores, axis=1, keepdims=True))
        weights = jnp.where(visible, jnp.exp(scores - row_max), 0.0)
        row_sum = lax.optimization_barrier(jnp.sum(weights, axis=1, keepdims=True))
        mixed = jnp.dot(weights.astype(jnp.bfloat16), value_head, preferred_element_type=jnp.float32)
        return (mixed / row_sum).astype(jnp.bfloat16)
    head_outputs = lax.map(one_head, jnp.arange(QUERY_HEADS, dtype=jnp.int32))
    attended = jnp.transpose(head_outputs, (1, 0, 2)).reshape(SEQUENCE_TOKENS, QUERY_HEADS * HEAD_SIZE)
    return jnp.dot(attended, out_weight, preferred_element_type=jnp.float32).astype(jnp.bfloat16)
```

```python
import math

import jax
import jax.numpy as jnp
from jax import lax
from jax.sharding import PartitionSpec as P

QUERY_HEADS = 32
KEY_VALUE_HEADS = 8
HEAD_SIZE = 128


def per_device(queries, keys, values, order, out_weight):
    row_count = queries.shape[0]
    local_groups = keys.shape[1] // HEAD_SIZE
    query_head_group = QUERY_HEADS // KEY_VALUE_HEADS
    score_scale = 1.0 / math.sqrt(HEAD_SIZE)
    first_row = lax.axis_index("context") * row_count
    query_pos = lax.dynamic_slice_in_dim(order, first_row, row_count, 0)
    stacked = queries.reshape(row_count, local_groups, query_head_group, HEAD_SIZE)
    stacked = stacked.transpose(1, 2, 0, 3).reshape(
        local_groups, query_head_group * row_count, HEAD_SIZE
    )
    stacked_pos = jnp.tile(query_pos, query_head_group)
    stacked_rows = query_head_group * row_count
    kv_part = lax.all_gather(
        jnp.concatenate([keys, values], axis=1), "context", axis=0, tiled=True
    )
    key_part = kv_part[:, : keys.shape[1]]
    value_part = kv_part[:, keys.shape[1] :]
    key_count = key_part.shape[0]
    running_max = jnp.full((local_groups, stacked_rows), -1e30, jnp.float32)
    key_heads = key_part.reshape(key_count, local_groups, HEAD_SIZE)
    value_heads = value_part.reshape(key_count, local_groups, HEAD_SIZE)
    scores = (
        jnp.einsum("grd,kgd->grk", stacked, key_heads, preferred_element_type=jnp.float32)
        * score_scale
    )
    visible = order[None, None, :] <= stacked_pos[None, :, None]
    scores = jnp.where(visible, scores, -1e30)
    new_max = jnp.maximum(running_max, jnp.max(scores, axis=2))
    weights = jnp.where(visible, jnp.exp(scores - new_max[..., None]), 0.0)
    new_sum = jnp.sum(weights, axis=2)
    product = jnp.einsum(
        "grk,kgd->grd",
        weights.astype(jnp.bfloat16),
        value_heads,
        preferred_element_type=jnp.float32,
    )
    attended = (product / new_sum[..., None]).astype(jnp.bfloat16)
    attended = attended.reshape(local_groups, query_head_group, row_count, HEAD_SIZE).transpose(
        2, 0, 1, 3
    )
    attended = attended.reshape(row_count, local_groups * query_head_group * HEAD_SIZE)
    partial_out = jnp.dot(
        attended,
        lax.all_gather(out_weight, "context", axis=1, tiled=True),
        preferred_element_type=jnp.float32,
    )
    return lax.psum_scatter(
        partial_out.astype(jnp.bfloat16), "tensor", scatter_dimension=1, tiled=True
    )


def solution(mesh):
    placed = (
        P(("dp", "context"), "tensor"),
        P(("dp", "context"), "tensor"),
        P(("dp", "context"), "tensor"),
        P("dp"),
        P("tensor", "context"),
    )
    return jax.shard_map(
        per_device,
        mesh=mesh,
        in_specs=placed,
        out_specs=P(("dp", "context"), "tensor"),
        check_vma=False,
    )
```

```python
import math

import jax
import jax.numpy as jnp
from jax import lax
from jax.sharding import PartitionSpec as P

QUERY_HEADS = 32
KEY_VALUE_HEADS = 8
HEAD_SIZE = 128


def exchange_gather(block, bits, axis_name, count):
    index = lax.axis_index(axis_name)
    stack = block[None]
    for bit in bits:
        received = lax.ppermute(stack, axis_name, [(i, i ^ bit) for i in range(count)])
        upper = (index & bit) != 0
        stack = jnp.where(
            upper,
            jnp.concatenate([received, stack], 0),
            jnp.concatenate([stack, received], 0),
        )
    return stack


def context_gather(block, context_size, low_first=True):
    bit_count = context_size.bit_length() - 1
    low = [1 << k for k in range(bit_count // 2)]
    high = [1 << k for k in range(bit_count // 2, bit_count)]
    if low_first:
        return exchange_gather(block, low + high, "context", context_size)
    stack = exchange_gather(block, high + low, "context", context_size)
    inner = 1 << len(high)
    stack = stack.reshape((context_size // inner, inner) + stack.shape[1:])
    stack = jnp.swapaxes(stack, 0, 1)
    return stack.reshape((context_size,) + stack.shape[2:])


def per_device(queries, keys, values, order, out_weight):
    row_count = queries.shape[0]
    local_groups = keys.shape[1] // HEAD_SIZE
    query_head_group = QUERY_HEADS // KEY_VALUE_HEADS
    score_scale = 1.0 / math.sqrt(HEAD_SIZE)
    context_size = lax.axis_size("context")
    dp_size = lax.axis_size("dp")

    core = lax.axis_index("dp") % 2
    weight_rows = out_weight.shape[0]
    half_rows = weight_rows // 2
    mine = lax.dynamic_slice_in_dim(out_weight, core * half_rows, half_rows, 0)
    quarter = half_rows // 2
    first = context_gather(mine[:quarter], context_size, True)
    second = context_gather(mine[quarter:], context_size, False)
    mine_all = jnp.concatenate([first, second], 1)
    other_all = lax.ppermute(mine_all, "dp", [(i, i ^ 1) for i in range(dp_size)])
    weight_all = jnp.where(
        core == 0,
        jnp.concatenate([mine_all, other_all], 1),
        jnp.concatenate([other_all, mine_all], 1),
    )

    first_row = lax.axis_index("context") * row_count
    query_pos = lax.dynamic_slice_in_dim(order, first_row, row_count, 0)
    stacked = queries.reshape(row_count, local_groups, query_head_group, HEAD_SIZE)
    stacked = stacked.transpose(1, 2, 0, 3).reshape(
        local_groups, query_head_group * row_count, HEAD_SIZE
    )
    stacked_pos = jnp.tile(query_pos, query_head_group)
    stacked_rows = query_head_group * row_count
    kv_part = context_gather(jnp.concatenate([keys, values], axis=1), context_size, True)
    kv_part = kv_part.reshape(context_size * row_count, keys.shape[1] + values.shape[1])
    key_part = kv_part[:, : keys.shape[1]]
    value_part = kv_part[:, keys.shape[1] :]
    key_count = key_part.shape[0]
    running_max = jnp.full((local_groups, stacked_rows), -1e30, jnp.float32)
    key_heads = key_part.reshape(key_count, local_groups, HEAD_SIZE)
    value_heads = value_part.reshape(key_count, local_groups, HEAD_SIZE)
    scores = (
        jnp.einsum("grd,kgd->grk", stacked, key_heads, preferred_element_type=jnp.float32)
        * score_scale
    )
    visible = order[None, None, :] <= stacked_pos[None, :, None]
    scores = jnp.where(visible, scores, -1e30)
    new_max = jnp.maximum(running_max, jnp.max(scores, axis=2))
    weights = jnp.where(visible, jnp.exp(scores - new_max[..., None]), 0.0)
    new_sum = jnp.sum(weights, axis=2)
    product = jnp.einsum(
        "grk,kgd->grd",
        weights.astype(jnp.bfloat16),
        value_heads,
        preferred_element_type=jnp.float32,
    )
    attended = (product / new_sum[..., None]).astype(jnp.bfloat16)
    attended = attended.reshape(local_groups, query_head_group, row_count, HEAD_SIZE).transpose(
        2, 0, 1, 3
    )
    attended = attended.reshape(row_count, local_groups * query_head_group * HEAD_SIZE)
    partial_out = jnp.einsum(
        "rh,chk->rck", attended, weight_all, preferred_element_type=jnp.float32
    ).reshape(row_count, -1)
    return lax.psum_scatter(
        partial_out.astype(jnp.bfloat16), "tensor", scatter_dimension=1, tiled=True
    )


def solution(mesh):
    placed = (
        P(("dp", "context"), "tensor"),
        P(("dp", "context"), "tensor"),
        P(("dp", "context"), "tensor"),
        P("dp"),
        P("tensor", "context"),
    )
    return jax.shard_map(
        per_device,
        mesh=mesh,
        in_specs=placed,
        out_specs=P(("dp", "context"), "tensor"),
        check_vma=False,
    )
```

```python
import math

import jax
import jax.numpy as jnp
from jax import lax
from jax.sharding import PartitionSpec as P

QUERY_HEADS = 32
KEY_VALUE_HEADS = 8
HEAD_SIZE = 128
X_SIZE = 4


def chain_plan(context_size, x_size, x_first_mask):
    y_bits = [x_size << k for k in range((context_size // x_size).bit_length() - 1)]
    steps = [(bit, bit) for bit in y_bits]
    if x_size == 4:
        steps += [(1, 1), (3, 2)] if x_first_mask == 1 else [(3, 2), (1, 3)]
    else:
        steps += [(1 << k, 1 << k) for k in range(x_size.bit_length() - 1)]
    return steps


def upper_of(index, mask):
    bits = index & mask
    parity = jnp.zeros_like(index)
    for k in range(mask.bit_length()):
        parity = parity ^ ((bits >> k) & 1)
    return parity != 0


def upper_static(index, mask):
    return bin(index & mask).count("1") % 2 == 1


def stacked_sources(context_size, steps):
    lists = [[c] for c in range(context_size)]
    for mask, side in steps:
        lists = [
            (lists[c ^ mask] + lists[c]) if upper_static(c, side) else (lists[c] + lists[c ^ mask])
            for c in range(context_size)
        ]
    assert all(entry == lists[0] for entry in lists)
    return lists[0]


def exchange_gather(block, steps, axis_name, count):
    index = lax.axis_index(axis_name)
    stack = block
    for mask, side in steps:
        received = lax.ppermute(stack, axis_name, [(i, i ^ mask) for i in range(count)])
        stack = jnp.where(
            upper_of(index, side),
            jnp.concatenate([received, stack], 1),
            jnp.concatenate([stack, received], 1),
        )
    return stack


def unpermute_blocks(product, sources, x_size):
    rows = product.shape[0]
    count = len(sources)
    y_count = count // x_size
    x_order = [sources[ix * y_count] for ix in range(x_size)]
    assert all(
        sources[ix * y_count + iy] == iy * x_size + x_order[ix]
        for ix in range(x_size)
        for iy in range(y_count)
    )
    product = product.reshape(rows, x_size, y_count, -1)
    inverse = [x_order.index(x) for x in range(x_size)]
    if inverse != list(range(x_size)):
        product = jnp.concatenate([product[:, i : i + 1] for i in inverse], axis=1)
    return jnp.swapaxes(product, 1, 2).reshape(rows, -1)


def per_device(queries, keys, values, order, out_weight):
    row_count = queries.shape[0]
    local_groups = keys.shape[1] // HEAD_SIZE
    query_head_group = QUERY_HEADS // KEY_VALUE_HEADS
    score_scale = 1.0 / math.sqrt(HEAD_SIZE)
    context_size = lax.axis_size("context")
    dp_size = lax.axis_size("dp")
    x_size = X_SIZE if context_size % X_SIZE == 0 and context_size > X_SIZE else 1

    core = lax.axis_index("dp") % 2
    weight_rows = out_weight.shape[0]
    half_rows = weight_rows // 2
    quarter = half_rows // 2
    mine = lax.dynamic_slice_in_dim(out_weight, core * half_rows, half_rows, 0)
    kv_width = keys.shape[1] + values.shape[1]
    steps_a = chain_plan(context_size, x_size, 1)
    steps_b = chain_plan(context_size, x_size, 3)
    block_a = jnp.concatenate([keys, values, mine[:quarter]], axis=1)[:, None, :]
    gathered_a = exchange_gather(block_a, steps_a, "context", context_size)
    gathered_b = exchange_gather(mine[quarter:][:, None, :], steps_b, "context", context_size)
    sources_a = stacked_sources(context_size, steps_a)
    sources_b = stacked_sources(context_size, steps_b)

    mine_weights = jnp.concatenate([gathered_a[:, :, kv_width:], gathered_b], axis=0)
    other_weights = lax.ppermute(mine_weights, "dp", [(i, i ^ 1) for i in range(dp_size)])

    kv_all = jnp.swapaxes(gathered_a[:, :, :kv_width], 0, 1).reshape(context_size * row_count, kv_width)
    key_pos = order.reshape(context_size, row_count)[jnp.array(sources_a)].reshape(-1)

    first_row = lax.axis_index("context") * row_count
    query_pos = lax.dynamic_slice_in_dim(order, first_row, row_count, 0)
    stacked = queries.reshape(row_count, local_groups, query_head_group, HEAD_SIZE)
    stacked = stacked.transpose(1, 2, 0, 3).reshape(
        local_groups, query_head_group * row_count, HEAD_SIZE
    )
    stacked_pos = jnp.tile(query_pos, query_head_group)
    stacked_rows = query_head_group * row_count
    key_part = kv_all[:, : keys.shape[1]]
    value_part = kv_all[:, keys.shape[1] :]
    key_count = key_part.shape[0]
    running_max = jnp.full((local_groups, stacked_rows), -1e30, jnp.float32)
    key_heads = key_part.reshape(key_count, local_groups, HEAD_SIZE)
    value_heads = value_part.reshape(key_count, local_groups, HEAD_SIZE)
    scores = (
        jnp.einsum("grd,kgd->grk", stacked, key_heads, preferred_element_type=jnp.float32)
        * score_scale
    )
    visible = key_pos[None, None, :] <= stacked_pos[None, :, None]
    scores = jnp.where(visible, scores, -1e30)
    new_max = jnp.maximum(running_max, jnp.max(scores, axis=2))
    weights = jnp.where(visible, jnp.exp(scores - new_max[..., None]), 0.0)
    new_sum = jnp.sum(weights, axis=2)
    product = jnp.einsum(
        "grk,kgd->grd",
        weights.astype(jnp.bfloat16),
        value_heads,
        preferred_element_type=jnp.float32,
    )
    attended = (product / new_sum[..., None]).astype(jnp.bfloat16)
    attended = attended.reshape(local_groups, query_head_group, row_count, HEAD_SIZE).transpose(
        2, 0, 1, 3
    )
    attended = attended.reshape(row_count, local_groups * query_head_group * HEAD_SIZE)

    total = None
    for piece, sources in ((0, sources_a), (1, sources_b)):
        mine_piece = mine_weights[piece * quarter : (piece + 1) * quarter]
        other_piece = other_weights[piece * quarter : (piece + 1) * quarter]
        low = jnp.where(core == 0, mine_piece, other_piece)
        high = jnp.where(core == 0, other_piece, mine_piece)
        piece_weight = jnp.concatenate([low, high], axis=0).reshape(2 * quarter, -1)
        piece_rows = jnp.concatenate(
            [
                attended[:, piece * quarter : (piece + 1) * quarter],
                attended[:, half_rows + piece * quarter : half_rows + (piece + 1) * quarter],
            ],
            axis=1,
        )
        product_out = jnp.dot(piece_rows, piece_weight, preferred_element_type=jnp.float32)
        product_out = unpermute_blocks(product_out, sources, x_size)
        total = product_out if total is None else total + product_out
    partial_out = total
    return lax.psum_scatter(
        partial_out.astype(jnp.bfloat16), "tensor", scatter_dimension=1, tiled=True
    )


def solution(mesh):
    placed = (
        P(("dp", "context"), "tensor"),
        P(("dp", "context"), "tensor"),
        P(("dp", "context"), "tensor"),
        P("dp"),
        P("tensor", "context"),
    )
    return jax.shard_map(
        per_device,
        mesh=mesh,
        in_specs=placed,
        out_specs=P(("dp", "context"), "tensor"),
        check_vma=False,
    )
```

```python
import math

import jax
import jax.numpy as jnp
from jax import lax
from jax.sharding import PartitionSpec as P

QUERY_HEADS = 32
KEY_VALUE_HEADS = 8
HEAD_SIZE = 128
X_SIZE = 4


def chain_plan(context_size, x_size, x_first_mask):
    y_bits = [x_size << k for k in range((context_size // x_size).bit_length() - 1)]
    steps = [(bit, bit) for bit in y_bits]
    if x_size == 4:
        steps += [(1, 1), (3, 2)] if x_first_mask == 1 else [(3, 2), (1, 3)]
    else:
        steps += [(1 << k, 1 << k) for k in range(x_size.bit_length() - 1)]
    return steps


def upper_of(index, mask):
    bits = index & mask
    parity = jnp.zeros_like(index)
    for k in range(mask.bit_length()):
        parity = parity ^ ((bits >> k) & 1)
    return parity != 0


def upper_static(index, mask):
    return bin(index & mask).count("1") % 2 == 1


def stacked_sources(context_size, steps):
    lists = [[c] for c in range(context_size)]
    for mask, side in steps:
        lists = [
            (lists[c ^ mask] + lists[c]) if upper_static(c, side) else (lists[c] + lists[c ^ mask])
            for c in range(context_size)
        ]
    assert all(entry == lists[0] for entry in lists)
    return lists[0]


def exchange_gather(block, steps, axis_name, count):
    index = lax.axis_index(axis_name)
    stack = block
    for mask, side in steps:
        received = lax.ppermute(stack, axis_name, [(i, i ^ mask) for i in range(count)])
        stack = jnp.where(
            upper_of(index, side),
            jnp.concatenate([received, stack], 1),
            jnp.concatenate([stack, received], 1),
        )
    return stack


def unpermute_blocks(product, sources, x_size):
    rows = product.shape[0]
    count = len(sources)
    y_count = count // x_size
    x_order = [sources[ix * y_count] for ix in range(x_size)]
    assert all(
        sources[ix * y_count + iy] == iy * x_size + x_order[ix]
        for ix in range(x_size)
        for iy in range(y_count)
    )
    product = product.reshape(rows, x_size, y_count, -1)
    inverse = [x_order.index(x) for x in range(x_size)]
    if inverse != list(range(x_size)):
        product = jnp.concatenate([product[:, i : i + 1] for i in inverse], axis=1)
    return jnp.swapaxes(product, 1, 2).reshape(rows, -1)


def per_device(queries, keys, values, order, out_weight):
    row_count = queries.shape[0]
    local_groups = keys.shape[1] // HEAD_SIZE
    query_head_group = QUERY_HEADS // KEY_VALUE_HEADS
    score_scale = 1.0 / math.sqrt(HEAD_SIZE)
    context_size = lax.axis_size("context")
    dp_size = lax.axis_size("dp")
    x_size = X_SIZE if context_size % X_SIZE == 0 and context_size > X_SIZE else 1

    core = lax.axis_index("dp") % 2
    weight_rows = out_weight.shape[0]
    half_rows = weight_rows // 2
    quarter = half_rows // 2
    mine = lax.dynamic_slice_in_dim(out_weight, core * half_rows, half_rows, 0)
    kv_width = keys.shape[1] + values.shape[1]
    steps_a = chain_plan(context_size, x_size, 1)
    steps_b = chain_plan(context_size, x_size, 3)
    block_a = jnp.concatenate([keys, values, mine[:quarter]], axis=1)[:, None, :]
    gathered_a = exchange_gather(block_a, steps_a, "context", context_size)
    gathered_b = exchange_gather(mine[quarter:][:, None, :], steps_b, "context", context_size)
    sources_a = stacked_sources(context_size, steps_a)
    sources_b = stacked_sources(context_size, steps_b)

    mine_weights = jnp.concatenate([gathered_a[:, :, kv_width:], gathered_b], axis=0)
    other_weights = lax.ppermute(mine_weights, "dp", [(i, i ^ 1) for i in range(dp_size)])

    kv_all = jnp.swapaxes(gathered_a[:, :, :kv_width], 0, 1).reshape(context_size * row_count, kv_width)
    key_pos = order.reshape(context_size, row_count)[jnp.array(sources_a)].reshape(-1)

    first_row = lax.axis_index("context") * row_count
    query_pos = lax.dynamic_slice_in_dim(order, first_row, row_count, 0)
    stacked = queries.reshape(row_count, local_groups, query_head_group, HEAD_SIZE)
    stacked = stacked.transpose(1, 2, 0, 3).reshape(
        local_groups, query_head_group * row_count, HEAD_SIZE
    )
    stacked_pos = jnp.tile(query_pos, query_head_group)
    stacked_rows = query_head_group * row_count
    key_part = kv_all[:, : keys.shape[1]]
    value_part = kv_all[:, keys.shape[1] :]
    key_count = key_part.shape[0]
    running_max = jnp.full((local_groups, stacked_rows), -1e30, jnp.float32)
    key_heads = key_part.reshape(key_count, local_groups, HEAD_SIZE)
    value_heads = value_part.reshape(key_count, local_groups, HEAD_SIZE)
    scores = (
        jnp.einsum("grd,kgd->grk", stacked, key_heads, preferred_element_type=jnp.float32)
        * score_scale
    )
    visible = key_pos[None, None, :] <= stacked_pos[None, :, None]
    scores = jnp.where(visible, scores, -1e30)
    new_max = jnp.maximum(running_max, jnp.max(scores, axis=2))
    weights = jnp.where(visible, jnp.exp(scores - new_max[..., None]), 0.0)
    new_sum = jnp.sum(weights, axis=2)
    product = jnp.einsum(
        "grk,kgd->grd",
        weights.astype(jnp.bfloat16),
        value_heads,
        preferred_element_type=jnp.float32,
    )
    attended = (product / new_sum[..., None]).astype(jnp.bfloat16)
    attended = attended.reshape(local_groups, query_head_group, row_count, HEAD_SIZE).transpose(
        2, 0, 1, 3
    )
    attended = attended.reshape(row_count, local_groups * query_head_group * HEAD_SIZE)

    total = None
    for piece, sources in ((0, sources_a), (1, sources_b)):
        mine_piece = mine_weights[piece * quarter : (piece + 1) * quarter]
        other_piece = other_weights[piece * quarter : (piece + 1) * quarter]
        low = jnp.where(core == 0, mine_piece, other_piece)
        high = jnp.where(core == 0, other_piece, mine_piece)
        piece_weight = jnp.concatenate([low, high], axis=0).reshape(2 * quarter, -1)
        piece_rows = jnp.concatenate(
            [
                attended[:, piece * quarter : (piece + 1) * quarter],
                attended[:, half_rows + piece * quarter : half_rows + (piece + 1) * quarter],
            ],
            axis=1,
        )
        product_out = jnp.dot(piece_rows, piece_weight, preferred_element_type=jnp.float32)
        product_out = unpermute_blocks(product_out, sources, x_size)
        total = product_out if total is None else total + product_out
    partial_out = total
    tensor_size = lax.axis_size("tensor")
    pieces = partial_out.astype(jnp.bfloat16).reshape(row_count, tensor_size, -1)
    pieces = lax.all_to_all(pieces, "tensor", 1, 1, tiled=True)
    return jnp.sum(pieces.astype(jnp.float32), axis=1).astype(jnp.bfloat16)


def solution(mesh):
    placed = (
        P(("dp", "context"), "tensor"),
        P(("dp", "context"), "tensor"),
        P(("dp", "context"), "tensor"),
        P("dp"),
        P("tensor", "context"),
    )
    return jax.shard_map(
        per_device,
        mesh=mesh,
        in_specs=placed,
        out_specs=P(("dp", "context"), "tensor"),
        check_vma=False,
    )
```

```python
import math

import jax
import jax.numpy as jnp
from jax import lax
from jax.sharding import PartitionSpec as P

QUERY_HEADS = 32
KEY_VALUE_HEADS = 8
HEAD_SIZE = 128
X_SIZE = 4


def chain_plan(context_size, x_size, x_first_mask):
    y_bits = [x_size << k for k in range((context_size // x_size).bit_length() - 1)]
    steps = [(bit, bit) for bit in y_bits]
    if x_size == 4:
        steps += [(1, 1), (3, 2)] if x_first_mask == 1 else [(3, 2), (1, 3)]
    else:
        steps += [(1 << k, 1 << k) for k in range(x_size.bit_length() - 1)]
    return steps


def upper_of(index, mask):
    bits = index & mask
    parity = jnp.zeros_like(index)
    for k in range(mask.bit_length()):
        parity = parity ^ ((bits >> k) & 1)
    return parity != 0


def upper_static(index, mask):
    return bin(index & mask).count("1") % 2 == 1


def stacked_sources(context_size, steps):
    lists = [[c] for c in range(context_size)]
    for mask, side in steps:
        lists = [
            (lists[c ^ mask] + lists[c]) if upper_static(c, side) else (lists[c] + lists[c ^ mask])
            for c in range(context_size)
        ]
    assert all(entry == lists[0] for entry in lists)
    return lists[0]


def exchange_gather(block, steps, axis_name, count):
    index = lax.axis_index(axis_name)
    stack = block
    for mask, side in steps:
        received = lax.ppermute(stack, axis_name, [(i, i ^ mask) for i in range(count)])
        stack = jnp.where(
            upper_of(index, side),
            jnp.concatenate([received, stack], 0),
            jnp.concatenate([stack, received], 0),
        )
    return stack


def per_device(queries, keys, values, order, out_weight):
    row_count = queries.shape[0]
    local_groups = keys.shape[1] // HEAD_SIZE
    query_head_group = QUERY_HEADS // KEY_VALUE_HEADS
    score_scale = 1.0 / math.sqrt(HEAD_SIZE)
    context_size = lax.axis_size("context")
    dp_size = lax.axis_size("dp")
    x_size = X_SIZE if context_size % X_SIZE == 0 and context_size > X_SIZE else 1

    core = lax.axis_index("dp") % 2
    weight_rows, weight_cols = out_weight.shape
    half_rows = weight_rows // 2
    mine = lax.dynamic_slice_in_dim(out_weight, core * half_rows, half_rows, 0)
    kv_width = keys.shape[1] + values.shape[1]
    steps = chain_plan(context_size, x_size, 1)
    sources = stacked_sources(context_size, steps)
    block = jnp.concatenate([keys, values, mine.reshape(row_count, -1)], axis=1)[None]
    stack = exchange_gather(block, steps, "context", context_size)

    weight_stack = stack[:, :, kv_width:].reshape(context_size, half_rows, weight_cols)
    mine_weights = jnp.concatenate(
        [weight_stack[sources.index(c)] for c in range(context_size)], axis=1
    )
    other_weights = lax.ppermute(mine_weights, "dp", [(i, i ^ 1) for i in range(dp_size)])
    weight_all = jnp.concatenate([mine_weights, other_weights], axis=0)

    kv_all = stack[:, :, :kv_width].reshape(context_size * row_count, kv_width)
    key_pos = order.reshape(context_size, row_count)[jnp.array(sources)].reshape(-1)

    first_row = lax.axis_index("context") * row_count
    query_pos = lax.dynamic_slice_in_dim(order, first_row, row_count, 0)
    stacked = queries.reshape(row_count, local_groups, query_head_group, HEAD_SIZE)
    stacked = stacked.transpose(1, 2, 0, 3).reshape(
        local_groups, query_head_group * row_count, HEAD_SIZE
    )
    stacked_pos = jnp.tile(query_pos, query_head_group)
    stacked_rows = query_head_group * row_count
    key_part = kv_all[:, : keys.shape[1]]
    value_part = kv_all[:, keys.shape[1] :]
    key_count = key_part.shape[0]
    running_max = jnp.full((local_groups, stacked_rows), -1e30, jnp.float32)
    key_heads = key_part.reshape(key_count, local_groups, HEAD_SIZE)
    value_heads = value_part.reshape(key_count, local_groups, HEAD_SIZE)
    scores = (
        jnp.einsum("grd,kgd->grk", stacked, key_heads, preferred_element_type=jnp.float32)
        * score_scale
    )
    visible = key_pos[None, None, :] <= stacked_pos[None, :, None]
    scores = jnp.where(visible, scores, -1e30)
    new_max = jnp.maximum(running_max, jnp.max(scores, axis=2))
    weights = jnp.where(visible, jnp.exp(scores - new_max[..., None]), 0.0)
    new_sum = jnp.sum(weights, axis=2)
    product = jnp.einsum(
        "grk,kgd->grd",
        weights.astype(jnp.bfloat16),
        value_heads,
        preferred_element_type=jnp.float32,
    )
    attended = (product / new_sum[..., None]).astype(jnp.bfloat16)
    attended = attended.reshape(local_groups, query_head_group, row_count, HEAD_SIZE).transpose(
        2, 0, 1, 3
    )
    attended = attended.reshape(row_count, local_groups * query_head_group * HEAD_SIZE)
    attended = jnp.concatenate(
        [
            lax.dynamic_slice_in_dim(attended, core * half_rows, half_rows, 1),
            lax.dynamic_slice_in_dim(attended, (1 - core) * half_rows, half_rows, 1),
        ],
        axis=1,
    )
    partial_out = jnp.dot(attended, weight_all, preferred_element_type=jnp.float32)

    tensor_size = lax.axis_size("tensor")
    pieces = partial_out.astype(jnp.bfloat16).reshape(row_count, tensor_size, -1)
    pieces = lax.all_to_all(pieces, "tensor", 1, 1, tiled=True)
    return jnp.sum(pieces.astype(jnp.float32), axis=1).astype(jnp.bfloat16)


def solution(mesh):
    placed = (
        P(("dp", "context"), "tensor"),
        P(("dp", "context"), "tensor"),
        P(("dp", "context"), "tensor"),
        P("dp"),
        P("tensor", "context"),
    )
    return jax.shard_map(
        per_device,
        mesh=mesh,
        in_specs=placed,
        out_specs=P(("dp", "context"), "tensor"),
        check_vma=False,
    )
```

```python
import math

import jax
import jax.numpy as jnp
from jax import lax
from jax.sharding import PartitionSpec as P

QUERY_HEADS = 32
KEY_VALUE_HEADS = 8
HEAD_SIZE = 128
X_SIZE = 4


def chain_plan(context_size, x_size, x_first_mask):
    y_bits = [x_size << k for k in range((context_size // x_size).bit_length() - 1)]
    steps = [(bit, bit) for bit in y_bits]
    if x_size == 4:
        steps += [(1, 1), (3, 2)] if x_first_mask == 1 else [(3, 2), (1, 3)]
    else:
        steps += [(1 << k, 1 << k) for k in range(x_size.bit_length() - 1)]
    return steps


def upper_of(index, mask):
    bits = index & mask
    parity = jnp.zeros_like(index)
    for k in range(mask.bit_length()):
        parity = parity ^ ((bits >> k) & 1)
    return parity != 0


def upper_static(index, mask):
    return bin(index & mask).count("1") % 2 == 1


def stacked_sources(context_size, steps):
    lists = [[c] for c in range(context_size)]
    for mask, side in steps:
        lists = [
            (lists[c ^ mask] + lists[c]) if upper_static(c, side) else (lists[c] + lists[c ^ mask])
            for c in range(context_size)
        ]
    assert all(entry == lists[0] for entry in lists)
    return lists[0]


def exchange_gather(block, steps, axis_name, count):
    index = lax.axis_index(axis_name)
    stack = block
    for mask, side in steps:
        received = lax.ppermute(stack, axis_name, [(i, i ^ mask) for i in range(count)])
        stack = jnp.where(
            upper_of(index, side),
            jnp.concatenate([received, stack], 1),
            jnp.concatenate([stack, received], 1),
        )
    return stack


def unpermute_blocks(product, sources, x_size):
    rows = product.shape[0]
    count = len(sources)
    y_count = count // x_size
    x_order = [sources[ix * y_count] for ix in range(x_size)]
    assert all(
        sources[ix * y_count + iy] == iy * x_size + x_order[ix]
        for ix in range(x_size)
        for iy in range(y_count)
    )
    product = product.reshape(rows, x_size, y_count, -1)
    inverse = [x_order.index(x) for x in range(x_size)]
    if inverse != list(range(x_size)):
        product = jnp.concatenate([product[:, i : i + 1] for i in inverse], axis=1)
    return jnp.swapaxes(product, 1, 2).reshape(rows, -1)


def per_device(queries, keys, values, order, out_weight):
    row_count = queries.shape[0]
    local_groups = keys.shape[1] // HEAD_SIZE
    query_head_group = QUERY_HEADS // KEY_VALUE_HEADS
    score_scale = 1.0 / math.sqrt(HEAD_SIZE)
    context_size = lax.axis_size("context")
    dp_size = lax.axis_size("dp")
    x_size = X_SIZE if context_size % X_SIZE == 0 and context_size > X_SIZE else 1

    core = lax.axis_index("dp") % 2
    weight_rows, weight_cols = out_weight.shape
    half_rows = weight_rows // 2
    quarter = half_rows // 2
    mine = lax.dynamic_slice_in_dim(out_weight, core * half_rows, half_rows, 0)
    kv_width = keys.shape[1] + values.shape[1]
    steps_a = chain_plan(context_size, x_size, 1)
    steps_b = chain_plan(context_size, x_size, 3)
    shared = 0
    while shared < min(len(steps_a), len(steps_b)) and steps_a[shared] == steps_b[shared]:
        shared += 1
    block = jnp.concatenate([keys, values, mine[:quarter], mine[quarter:]], axis=1)[:, None, :]
    gathered = exchange_gather(block, steps_a[:shared], "context", context_size)
    gathered_a = exchange_gather(
        gathered[:, :, : kv_width + weight_cols], steps_a[shared:], "context", context_size
    )
    gathered_b = exchange_gather(
        gathered[:, :, kv_width + weight_cols :], steps_b[shared:], "context", context_size
    )
    sources_a = stacked_sources(context_size, steps_a)
    sources_b = stacked_sources(context_size, steps_b)

    mine_weights = jnp.concatenate([gathered_a[:, :, kv_width:], gathered_b], axis=0)
    other_weights = lax.ppermute(mine_weights, "dp", [(i, i ^ 1) for i in range(dp_size)])

    kv_all = jnp.swapaxes(gathered_a[:, :, :kv_width], 0, 1).reshape(context_size * row_count, kv_width)
    key_pos = order.reshape(context_size, row_count)[jnp.array(sources_a)].reshape(-1)

    first_row = lax.axis_index("context") * row_count
    query_pos = lax.dynamic_slice_in_dim(order, first_row, row_count, 0)
    stacked = queries.reshape(row_count, local_groups, query_head_group, HEAD_SIZE)
    stacked = stacked.transpose(1, 2, 0, 3).reshape(
        local_groups, query_head_group * row_count, HEAD_SIZE
    )
    stacked_pos = jnp.tile(query_pos, query_head_group)
    stacked_rows = query_head_group * row_count
    key_part = kv_all[:, : keys.shape[1]]
    value_part = kv_all[:, keys.shape[1] :]
    key_count = key_part.shape[0]
    running_max = jnp.full((local_groups, stacked_rows), -1e30, jnp.float32)
    key_heads = key_part.reshape(key_count, local_groups, HEAD_SIZE)
    value_heads = value_part.reshape(key_count, local_groups, HEAD_SIZE)
    scores = (
        jnp.einsum("grd,kgd->grk", stacked, key_heads, preferred_element_type=jnp.float32)
        * score_scale
    )
    visible = key_pos[None, None, :] <= stacked_pos[None, :, None]
    scores = jnp.where(visible, scores, -1e30)
    new_max = jnp.maximum(running_max, jnp.max(scores, axis=2))
    weights = jnp.where(visible, jnp.exp(scores - new_max[..., None]), 0.0)
    new_sum = jnp.sum(weights, axis=2)
    product = jnp.einsum(
        "grk,kgd->grd",
        weights.astype(jnp.bfloat16),
        value_heads,
        preferred_element_type=jnp.float32,
    )
    attended = (product / new_sum[..., None]).astype(jnp.bfloat16)
    attended = attended.reshape(local_groups, query_head_group, row_count, HEAD_SIZE).transpose(
        2, 0, 1, 3
    )
    attended = attended.reshape(row_count, local_groups * query_head_group * HEAD_SIZE)

    total = None
    for piece, sources in ((0, sources_a), (1, sources_b)):
        mine_piece = mine_weights[piece * quarter : (piece + 1) * quarter]
        other_piece = other_weights[piece * quarter : (piece + 1) * quarter]
        piece_weight = jnp.concatenate([mine_piece, other_piece], axis=0).reshape(2 * quarter, -1)
        piece_rows = jnp.concatenate(
            [
                lax.dynamic_slice_in_dim(attended, core * half_rows + piece * quarter, quarter, 1),
                lax.dynamic_slice_in_dim(
                    attended, (1 - core) * half_rows + piece * quarter, quarter, 1
                ),
            ],
            axis=1,
        )
        product_out = jnp.dot(piece_rows, piece_weight, preferred_element_type=jnp.float32)
        product_out = unpermute_blocks(product_out, sources, x_size)
        total = product_out if total is None else total + product_out
    partial_out = total
    tensor_size = lax.axis_size("tensor")
    pieces = partial_out.astype(jnp.bfloat16).reshape(row_count, tensor_size, -1)
    pieces = lax.all_to_all(pieces, "tensor", 1, 1, tiled=True)
    return jnp.sum(pieces.astype(jnp.float32), axis=1).astype(jnp.bfloat16)


def solution(mesh):
    placed = (
        P(("dp", "context"), "tensor"),
        P(("dp", "context"), "tensor"),
        P(("dp", "context"), "tensor"),
        P("dp"),
        P("tensor", "context"),
    )
    return jax.shard_map(
        per_device,
        mesh=mesh,
        in_specs=placed,
        out_specs=P(("dp", "context"), "tensor"),
        check_vma=False,
    )
```

```python
import math

import jax
import jax.numpy as jnp
from jax import lax
from jax.sharding import PartitionSpec as P

QUERY_HEADS = 32
KEY_VALUE_HEADS = 8
HEAD_SIZE = 128
X_SIZE = 4


def chain_plan(context_size, x_size, x_first_mask):
    y_bits = [x_size << k for k in range((context_size // x_size).bit_length() - 1)]
    steps = [(bit, bit) for bit in y_bits]
    if x_size == 4:
        steps += [(1, 1), (3, 2)] if x_first_mask == 1 else [(3, 2), (1, 3)]
    else:
        steps += [(1 << k, 1 << k) for k in range(x_size.bit_length() - 1)]
    return steps


def upper_of(index, mask):
    bits = index & mask
    parity = jnp.zeros_like(index)
    for k in range(mask.bit_length()):
        parity = parity ^ ((bits >> k) & 1)
    return parity != 0


def upper_static(index, mask):
    return bin(index & mask).count("1") % 2 == 1


def stacked_sources(context_size, steps):
    lists = [[c] for c in range(context_size)]
    for mask, side in steps:
        lists = [
            (lists[c ^ mask] + lists[c]) if upper_static(c, side) else (lists[c] + lists[c ^ mask])
            for c in range(context_size)
        ]
    assert all(entry == lists[0] for entry in lists)
    return lists[0]


def exchange_gather(block, steps, axis_name, count):
    index = lax.axis_index(axis_name)
    stack = block
    for mask, side in steps:
        received = lax.ppermute(stack, axis_name, [(i, i ^ mask) for i in range(count)])
        stack = jnp.where(
            upper_of(index, side),
            jnp.concatenate([received, stack], 1),
            jnp.concatenate([stack, received], 1),
        )
    return stack


def unpermute_blocks(product, sources, x_size):
    rows = product.shape[0]
    count = len(sources)
    y_count = count // x_size
    x_order = [sources[ix * y_count] for ix in range(x_size)]
    assert all(
        sources[ix * y_count + iy] == iy * x_size + x_order[ix]
        for ix in range(x_size)
        for iy in range(y_count)
    )
    product = product.reshape(rows, x_size, y_count, -1)
    inverse = [x_order.index(x) for x in range(x_size)]
    if inverse != list(range(x_size)):
        product = jnp.concatenate([product[:, i : i + 1] for i in inverse], axis=1)
    return jnp.swapaxes(product, 1, 2).reshape(rows, -1)


def restack(stack, sources, target, x_size):
    rows, count = stack.shape[:2]
    y_count = count // x_size
    x_from = [sources[ix * y_count] for ix in range(x_size)]
    x_to = [target[ix * y_count] for ix in range(x_size)]
    assert all(
        sources[ix * y_count + iy] - x_from[ix] == target[ix * y_count + iy] - x_to[ix]
        for ix in range(x_size)
        for iy in range(y_count)
    )
    picks = [x_from.index(x) for x in x_to]
    if picks == list(range(x_size)):
        return stack
    stack = stack.reshape(rows, x_size, y_count, -1)
    stack = jnp.concatenate([stack[:, i : i + 1] for i in picks], axis=1)
    return stack.reshape(rows, count, -1)


def per_device(queries, keys, values, order, out_weight):
    row_count = queries.shape[0]
    local_groups = keys.shape[1] // HEAD_SIZE
    query_head_group = QUERY_HEADS // KEY_VALUE_HEADS
    score_scale = 1.0 / math.sqrt(HEAD_SIZE)
    context_size = lax.axis_size("context")
    dp_size = lax.axis_size("dp")
    x_size = X_SIZE if context_size % X_SIZE == 0 and context_size > X_SIZE else 1

    core = lax.axis_index("dp") % 2
    weight_rows, weight_cols = out_weight.shape
    half_rows = weight_rows // 2
    quarter = half_rows // 2
    mine = lax.dynamic_slice_in_dim(out_weight, core * half_rows, half_rows, 0)
    steps_a = chain_plan(context_size, x_size, 1)
    steps_b = chain_plan(context_size, x_size, 3)
    shared = 0
    while shared < min(len(steps_a), len(steps_b)) and steps_a[shared] == steps_b[shared]:
        shared += 1
    key_width = keys.shape[1]
    block = jnp.concatenate([keys, mine[:quarter], values, mine[quarter:]], axis=1)[:, None, :]
    gathered = exchange_gather(block, steps_a[:shared], "context", context_size)
    gathered_a = exchange_gather(
        gathered[:, :, : key_width + weight_cols], steps_a[shared:], "context", context_size
    )
    gathered_b = exchange_gather(
        gathered[:, :, key_width + weight_cols :], steps_b[shared:], "context", context_size
    )
    sources_a = stacked_sources(context_size, steps_a)
    sources_b = stacked_sources(context_size, steps_b)

    mine_weights = jnp.concatenate(
        [gathered_a[:, :, key_width:], gathered_b[:, :, values.shape[1] :]], axis=0
    )
    other_weights = lax.ppermute(mine_weights, "dp", [(i, i ^ 1) for i in range(dp_size)])

    key_stack = gathered_a[:, :, :key_width]
    value_stack = restack(gathered_b[:, :, : values.shape[1]], sources_b, sources_a, x_size)
    key_part = jnp.swapaxes(key_stack, 0, 1).reshape(context_size * row_count, key_width)
    value_part = jnp.swapaxes(value_stack, 0, 1).reshape(context_size * row_count, -1)
    key_pos = order.reshape(context_size, row_count)[jnp.array(sources_a)].reshape(-1)

    first_row = lax.axis_index("context") * row_count
    query_pos = lax.dynamic_slice_in_dim(order, first_row, row_count, 0)
    stacked = queries.reshape(row_count, local_groups, query_head_group, HEAD_SIZE)
    stacked = stacked.transpose(1, 2, 0, 3).reshape(
        local_groups, query_head_group * row_count, HEAD_SIZE
    )
    stacked_pos = jnp.tile(query_pos, query_head_group)
    stacked_rows = query_head_group * row_count
    key_count = key_part.shape[0]
    running_max = jnp.full((local_groups, stacked_rows), -1e30, jnp.float32)
    key_heads = key_part.reshape(key_count, local_groups, HEAD_SIZE)
    value_heads = value_part.reshape(key_count, local_groups, HEAD_SIZE)
    scores = (
        jnp.einsum("grd,kgd->grk", stacked, key_heads, preferred_element_type=jnp.float32)
        * score_scale
    )
    visible = key_pos[None, None, :] <= stacked_pos[None, :, None]
    scores = jnp.where(visible, scores, -1e30)
    new_max = jnp.maximum(running_max, jnp.max(scores, axis=2))
    weights = jnp.where(visible, jnp.exp(scores - new_max[..., None]), 0.0)
    new_sum = jnp.sum(weights, axis=2)
    product = jnp.einsum(
        "grk,kgd->grd",
        weights.astype(jnp.bfloat16),
        value_heads,
        preferred_element_type=jnp.float32,
    )
    attended = (product / new_sum[..., None]).astype(jnp.bfloat16)
    attended = attended.reshape(local_groups, query_head_group, row_count, HEAD_SIZE).transpose(
        2, 0, 1, 3
    )
    attended = attended.reshape(row_count, local_groups * query_head_group * HEAD_SIZE)

    total = None
    for piece, sources in ((0, sources_a), (1, sources_b)):
        mine_piece = mine_weights[piece * quarter : (piece + 1) * quarter]
        other_piece = other_weights[piece * quarter : (piece + 1) * quarter]
        piece_weight = jnp.concatenate([mine_piece, other_piece], axis=0).reshape(2 * quarter, -1)
        piece_rows = jnp.concatenate(
            [
                lax.dynamic_slice_in_dim(attended, core * half_rows + piece * quarter, quarter, 1),
                lax.dynamic_slice_in_dim(
                    attended, (1 - core) * half_rows + piece * quarter, quarter, 1
                ),
            ],
            axis=1,
        )
        product_out = jnp.dot(piece_rows, piece_weight, preferred_element_type=jnp.float32)
        product_out = unpermute_blocks(product_out, sources, x_size)
        total = product_out if total is None else total + product_out
    partial_out = total
    tensor_size = lax.axis_size("tensor")
    pieces = partial_out.astype(jnp.bfloat16).reshape(row_count, tensor_size, -1)
    pieces = lax.all_to_all(pieces, "tensor", 1, 1, tiled=True)
    return jnp.sum(pieces.astype(jnp.float32), axis=1).astype(jnp.bfloat16)


def solution(mesh):
    placed = (
        P(("dp", "context"), "tensor"),
        P(("dp", "context"), "tensor"),
        P(("dp", "context"), "tensor"),
        P("dp"),
        P("tensor", "context"),
    )
    return jax.shard_map(
        per_device,
        mesh=mesh,
        in_specs=placed,
        out_specs=P(("dp", "context"), "tensor"),
        check_vma=False,
    )
```

```python
import math

import jax
import jax.numpy as jnp
from jax import lax
from jax.sharding import PartitionSpec as P

QUERY_HEADS = 32
KEY_VALUE_HEADS = 8
HEAD_SIZE = 128
X_SIZE = 4


def chain_plan(context_size, x_size, x_first_mask):
    y_bits = [x_size << k for k in range((context_size // x_size).bit_length() - 1)]
    steps = [(bit, bit) for bit in y_bits]
    if x_size == 4:
        steps += [(1, 1), (3, 2)] if x_first_mask == 1 else [(3, 2), (1, 3)]
    else:
        steps += [(1 << k, 1 << k) for k in range(x_size.bit_length() - 1)]
    return steps


def upper_of(index, mask):
    bits = index & mask
    parity = jnp.zeros_like(index)
    for k in range(mask.bit_length()):
        parity = parity ^ ((bits >> k) & 1)
    return parity != 0


def upper_static(index, mask):
    return bin(index & mask).count("1") % 2 == 1


def stacked_sources(context_size, steps):
    lists = [[c] for c in range(context_size)]
    for mask, side in steps:
        lists = [
            (lists[c ^ mask] + lists[c]) if upper_static(c, side) else (lists[c] + lists[c ^ mask])
            for c in range(context_size)
        ]
    assert all(entry == lists[0] for entry in lists)
    return lists[0]


def exchange_gather(block, steps, axis_name, count):
    index = lax.axis_index(axis_name)
    stack = block
    for mask, side in steps:
        received = lax.ppermute(stack, axis_name, [(i, i ^ mask) for i in range(count)])
        stack = jnp.where(
            upper_of(index, side),
            jnp.concatenate([received, stack], 1),
            jnp.concatenate([stack, received], 1),
        )
    return stack


def unpermute_blocks(product, sources, x_size):
    rows = product.shape[0]
    count = len(sources)
    y_count = count // x_size
    x_order = [sources[ix * y_count] for ix in range(x_size)]
    assert all(
        sources[ix * y_count + iy] == iy * x_size + x_order[ix]
        for ix in range(x_size)
        for iy in range(y_count)
    )
    product = product.reshape(rows, x_size, y_count, -1)
    inverse = [x_order.index(x) for x in range(x_size)]
    if inverse != list(range(x_size)):
        product = jnp.concatenate([product[:, i : i + 1] for i in inverse], axis=1)
    return jnp.swapaxes(product, 1, 2).reshape(rows, -1)


def restack(stack, sources, target, x_size):
    rows, count = stack.shape[:2]
    y_count = count // x_size
    x_from = [sources[ix * y_count] for ix in range(x_size)]
    x_to = [target[ix * y_count] for ix in range(x_size)]
    assert all(
        sources[ix * y_count + iy] - x_from[ix] == target[ix * y_count + iy] - x_to[ix]
        for ix in range(x_size)
        for iy in range(y_count)
    )
    picks = [x_from.index(x) for x in x_to]
    if picks == list(range(x_size)):
        return stack
    stack = stack.reshape(rows, x_size, y_count, -1)
    stack = jnp.concatenate([stack[:, i : i + 1] for i in picks], axis=1)
    return stack.reshape(rows, count, -1)


def per_device(queries, keys, values, order, out_weight):
    row_count = queries.shape[0]
    local_groups = keys.shape[1] // HEAD_SIZE
    query_head_group = QUERY_HEADS // KEY_VALUE_HEADS
    score_scale = 1.0 / math.sqrt(HEAD_SIZE)
    context_size = lax.axis_size("context")
    dp_size = lax.axis_size("dp")
    x_size = X_SIZE if context_size % X_SIZE == 0 and context_size > X_SIZE else 1

    core = lax.axis_index("dp") % 2
    weight_rows, weight_cols = out_weight.shape
    half_rows = weight_rows // 2
    quarter = half_rows // 2
    mine = lax.dynamic_slice_in_dim(out_weight, core * half_rows, half_rows, 0)
    steps_a = chain_plan(context_size, x_size, 1)
    steps_b = chain_plan(context_size, x_size, 3)
    shared = 0
    while shared < min(len(steps_a), len(steps_b)) and steps_a[shared] == steps_b[shared]:
        shared += 1
    key_width = keys.shape[1]
    quarters = [
        mine[k * quarter : (k + 1) * quarter].T.reshape(row_count, -1) for k in range(2)
    ]
    block = jnp.concatenate([keys, quarters[0], values, quarters[1]], axis=1)[:, None, :]
    gathered = exchange_gather(block, steps_a[:shared], "context", context_size)
    gathered_a = exchange_gather(
        gathered[:, :, : key_width + weight_cols], steps_a[shared:], "context", context_size
    )
    gathered_b = exchange_gather(
        gathered[:, :, key_width + weight_cols :], steps_b[shared:], "context", context_size
    )
    sources_a = stacked_sources(context_size, steps_a)
    sources_b = stacked_sources(context_size, steps_b)

    mine_weights = jnp.concatenate(
        [gathered_a[:, :, key_width:], gathered_b[:, :, values.shape[1] :]], axis=0
    )
    other_weights = lax.ppermute(mine_weights, "dp", [(i, i ^ 1) for i in range(dp_size)])

    key_stack = gathered_a[:, :, :key_width]
    value_stack = restack(gathered_b[:, :, : values.shape[1]], sources_b, sources_a, x_size)
    key_part = jnp.swapaxes(key_stack, 0, 1).reshape(context_size * row_count, key_width)
    value_part = jnp.swapaxes(value_stack, 0, 1).reshape(context_size * row_count, -1)
    key_pos = order.reshape(context_size, row_count)[jnp.array(sources_a)].reshape(-1)

    first_row = lax.axis_index("context") * row_count
    query_pos = lax.dynamic_slice_in_dim(order, first_row, row_count, 0)
    stacked = queries.reshape(row_count, local_groups, query_head_group, HEAD_SIZE)
    stacked = stacked.transpose(1, 2, 0, 3).reshape(
        local_groups, query_head_group * row_count, HEAD_SIZE
    )
    stacked_pos = jnp.tile(query_pos, query_head_group)
    stacked_rows = query_head_group * row_count
    key_count = key_part.shape[0]
    running_max = jnp.full((local_groups, stacked_rows), -1e30, jnp.float32)
    key_heads = key_part.reshape(key_count, local_groups, HEAD_SIZE)
    value_heads = value_part.reshape(key_count, local_groups, HEAD_SIZE)
    scores = (
        jnp.einsum("grd,kgd->grk", stacked, key_heads, preferred_element_type=jnp.float32)
        * score_scale
    )
    visible = key_pos[None, None, :] <= stacked_pos[None, :, None]
    scores = jnp.where(visible, scores, -1e30)
    new_max = jnp.maximum(running_max, jnp.max(scores, axis=2))
    weights = jnp.where(visible, jnp.exp(scores - new_max[..., None]), 0.0)
    new_sum = jnp.sum(weights, axis=2)
    product = jnp.einsum(
        "grk,kgd->grd",
        weights.astype(jnp.bfloat16),
        value_heads,
        preferred_element_type=jnp.float32,
    )
    attended = (product / new_sum[..., None]).astype(jnp.bfloat16)
    attended = attended.reshape(local_groups, query_head_group, row_count, HEAD_SIZE).transpose(
        2, 0, 1, 3
    )
    attended = attended.reshape(row_count, local_groups * query_head_group * HEAD_SIZE)

    total = None
    for piece, sources in ((0, sources_a), (1, sources_b)):
        for which, held in ((0, mine_weights), (1, other_weights)):
            piece_t = held[piece * row_count : (piece + 1) * row_count]
            piece_t = jnp.swapaxes(piece_t, 0, 1).reshape(context_size, weight_cols, quarter)
            owner = core if which == 0 else 1 - core
            piece_rows = lax.dynamic_slice_in_dim(
                attended, owner * half_rows + piece * quarter, quarter, 1
            )
            product_out = jnp.einsum(
                "rh,nkh->rnk", piece_rows, piece_t, preferred_element_type=jnp.float32
            ).reshape(row_count, -1)
            product_out = unpermute_blocks(product_out, sources, x_size)
            total = product_out if total is None else total + product_out
    partial_out = total
    tensor_size = lax.axis_size("tensor")
    pieces = partial_out.astype(jnp.bfloat16).reshape(row_count, tensor_size, -1)
    pieces = lax.all_to_all(pieces, "tensor", 1, 1, tiled=True)
    return jnp.sum(pieces.astype(jnp.float32), axis=1).astype(jnp.bfloat16)


def solution(mesh):
    placed = (
        P(("dp", "context"), "tensor"),
        P(("dp", "context"), "tensor"),
        P(("dp", "context"), "tensor"),
        P("dp"),
        P("tensor", "context"),
    )
    return jax.shard_map(
        per_device,
        mesh=mesh,
        in_specs=placed,
        out_specs=P(("dp", "context"), "tensor"),
        check_vma=False,
    )
```

```python
import math

import jax
import jax.numpy as jnp
from jax import lax
from jax.sharding import PartitionSpec as P

QUERY_HEADS = 32
KEY_VALUE_HEADS = 8
HEAD_SIZE = 128
X_SIZE = 4


def chain_plan(context_size, x_size, x_first_mask):
    y_bits = [x_size << k for k in range((context_size // x_size).bit_length() - 1)][::-1]
    steps = [(bit, bit) for bit in y_bits]
    if x_size == 4:
        steps += [(1, 1), (3, 2)] if x_first_mask == 1 else [(3, 2), (1, 3)]
    else:
        steps += [(1 << k, 1 << k) for k in range(x_size.bit_length() - 1)]
    return steps


def upper_of(index, mask):
    bits = index & mask
    parity = jnp.zeros_like(index)
    for k in range(mask.bit_length()):
        parity = parity ^ ((bits >> k) & 1)
    return parity != 0


def upper_static(index, mask):
    return bin(index & mask).count("1") % 2 == 1


def stacked_sources(context_size, steps):
    lists = [[c] for c in range(context_size)]
    for mask, side in steps:
        lists = [
            (lists[c ^ mask] + lists[c]) if upper_static(c, side) else (lists[c] + lists[c ^ mask])
            for c in range(context_size)
        ]
    assert all(entry == lists[0] for entry in lists)
    return lists[0]


def exchange_gather(block, steps, axis_name, count):
    index = lax.axis_index(axis_name)
    stack = block
    for mask, side in steps:
        received = lax.ppermute(stack, axis_name, [(i, i ^ mask) for i in range(count)])
        stack = jnp.where(
            upper_of(index, side),
            jnp.concatenate([received, stack], 1),
            jnp.concatenate([stack, received], 1),
        )
    return stack


def unpermute_blocks(product, sources, x_size):
    rows, count = product.shape[:2]
    y_count = count // x_size
    x_order = [sources[ix * y_count] % x_size for ix in range(x_size)]
    y_order = [sources[iy] // x_size for iy in range(y_count)]
    assert all(
        sources[ix * y_count + iy] == y_order[iy] * x_size + x_order[ix]
        for ix in range(x_size)
        for iy in range(y_count)
    )
    product = product.reshape(rows, x_size, y_count, -1)
    x_inverse = [x_order.index(x) for x in range(x_size)]
    y_inverse = [y_order.index(y) for y in range(y_count)]
    if x_inverse != list(range(x_size)):
        product = jnp.concatenate([product[:, i : i + 1] for i in x_inverse], axis=1)
    if y_inverse != list(range(y_count)):
        product = jnp.concatenate([product[:, :, i : i + 1] for i in y_inverse], axis=2)
    return jnp.swapaxes(product, 1, 2).reshape(rows, count, -1)


def restack(stack, sources, target, x_size):
    rows, count = stack.shape[:2]
    y_count = count // x_size
    x_from = [sources[ix * y_count] for ix in range(x_size)]
    x_to = [target[ix * y_count] for ix in range(x_size)]
    assert all(
        sources[ix * y_count + iy] - x_from[ix] == target[ix * y_count + iy] - x_to[ix]
        for ix in range(x_size)
        for iy in range(y_count)
    )
    picks = [x_from.index(x) for x in x_to]
    if picks == list(range(x_size)):
        return stack
    stack = stack.reshape(rows, x_size, y_count, -1)
    stack = jnp.concatenate([stack[:, i : i + 1] for i in picks], axis=1)
    return stack.reshape(rows, count, -1)


def per_device(queries, keys, values, order, out_weight):
    row_count = queries.shape[0]
    local_groups = keys.shape[1] // HEAD_SIZE
    query_head_group = QUERY_HEADS // KEY_VALUE_HEADS
    score_scale = 1.0 / math.sqrt(HEAD_SIZE)
    context_size = lax.axis_size("context")
    dp_size = lax.axis_size("dp")
    x_size = X_SIZE if context_size % X_SIZE == 0 and context_size > X_SIZE else 1

    core = lax.axis_index("dp") % 2
    weight_rows, weight_cols = out_weight.shape
    half_rows = weight_rows // 2
    quarter = half_rows // 2
    mine = lax.dynamic_slice_in_dim(out_weight, core * half_rows, half_rows, 0)
    steps_a = chain_plan(context_size, x_size, 1)
    steps_b = chain_plan(context_size, x_size, 3)
    shared = 0
    while shared < min(len(steps_a), len(steps_b)) and steps_a[shared] == steps_b[shared]:
        shared += 1
    key_width = keys.shape[1]
    quarters = [
        mine[k * quarter : (k + 1) * quarter].T.reshape(row_count, -1) for k in range(2)
    ]
    block = jnp.concatenate([keys, quarters[0], values, quarters[1]], axis=1)[:, None, :]
    gathered = exchange_gather(block, steps_a[:shared], "context", context_size)
    gathered_a = exchange_gather(
        gathered[:, :, : key_width + weight_cols], steps_a[shared:], "context", context_size
    )
    gathered_b = exchange_gather(
        gathered[:, :, key_width + weight_cols :], steps_b[shared:], "context", context_size
    )
    sources_a = stacked_sources(context_size, steps_a)
    sources_b = stacked_sources(context_size, steps_b)

    mine_weights = jnp.concatenate(
        [gathered_a[:, :, key_width:], gathered_b[:, :, values.shape[1] :]], axis=1
    )
    other_weights = lax.ppermute(mine_weights, "dp", [(i, i ^ 1) for i in range(dp_size)])

    key_stack = gathered_a[:, :, :key_width]
    value_stack = restack(gathered_b[:, :, : values.shape[1]], sources_b, sources_a, x_size)
    key_part = jnp.swapaxes(key_stack, 0, 1).reshape(context_size * row_count, key_width)
    value_part = jnp.swapaxes(value_stack, 0, 1).reshape(context_size * row_count, -1)
    key_pos = order.reshape(context_size, row_count)[jnp.array(sources_a)].reshape(-1)

    first_row = lax.axis_index("context") * row_count
    query_pos = lax.dynamic_slice_in_dim(order, first_row, row_count, 0)
    stacked = queries.reshape(row_count, local_groups, query_head_group, HEAD_SIZE)
    stacked = stacked.transpose(1, 2, 0, 3).reshape(
        local_groups, query_head_group * row_count, HEAD_SIZE
    )
    stacked_pos = jnp.tile(query_pos, query_head_group)
    stacked_rows = query_head_group * row_count
    key_count = key_part.shape[0]
    running_max = jnp.full((local_groups, stacked_rows), -1e30, jnp.float32)
    key_heads = key_part.reshape(key_count, local_groups, HEAD_SIZE)
    value_heads = value_part.reshape(key_count, local_groups, HEAD_SIZE)
    scores = (
        jnp.einsum("grd,kgd->grk", stacked, key_heads, preferred_element_type=jnp.float32)
        * score_scale
    )
    visible = key_pos[None, None, :] <= stacked_pos[None, :, None]
    scores = jnp.where(visible, scores, -1e30)
    new_max = jnp.maximum(running_max, jnp.max(scores, axis=2))
    weights = jnp.where(visible, jnp.exp(scores - new_max[..., None]), 0.0)
    new_sum = jnp.sum(weights, axis=2)
    product = jnp.einsum(
        "grk,kgd->grd",
        weights.astype(jnp.bfloat16),
        value_heads,
        preferred_element_type=jnp.float32,
    )
    attended = (product / new_sum[..., None]).astype(jnp.bfloat16)
    attended = attended.reshape(local_groups, query_head_group, row_count, HEAD_SIZE).transpose(
        2, 0, 1, 3
    )
    attended = attended.reshape(row_count, local_groups * query_head_group * HEAD_SIZE)

    total = None
    for piece, sources in ((0, sources_a), (1, sources_b)):
        for which, held in ((0, mine_weights), (1, other_weights)):
            piece_t = held[:, piece * context_size : (piece + 1) * context_size]
            piece_t = jnp.swapaxes(piece_t, 0, 1).reshape(context_size, weight_cols, quarter)
            owner = core if which == 0 else 1 - core
            piece_rows = lax.dynamic_slice_in_dim(
                attended, owner * half_rows + piece * quarter, quarter, 1
            )
            product_out = jnp.einsum(
                "rh,nkh->rnk", piece_rows, piece_t, preferred_element_type=jnp.float32
            )
            product_out = unpermute_blocks(product_out, sources, x_size)
            total = product_out if total is None else total + product_out
    tensor_size = lax.axis_size("tensor")
    pieces = total.astype(jnp.bfloat16).reshape(row_count, tensor_size, -1)
    pieces = jnp.swapaxes(pieces, 0, 1)
    pieces = lax.all_to_all(pieces, "tensor", 0, 0, tiled=True)
    return jnp.sum(pieces.astype(jnp.float32), axis=0).astype(jnp.bfloat16)


def solution(mesh):
    placed = (
        P(("dp", "context"), "tensor"),
        P(("dp", "context"), "tensor"),
        P(("dp", "context"), "tensor"),
        P("dp"),
        P("tensor", "context"),
    )
    return jax.shard_map(
        per_device,
        mesh=mesh,
        in_specs=placed,
        out_specs=P(("dp", "context"), "tensor"),
        check_vma=False,
    )
```

```python
import math

import jax
import jax.numpy as jnp
from jax import lax
from jax.sharding import PartitionSpec as P

QUERY_HEADS = 32
KEY_VALUE_HEADS = 8
HEAD_SIZE = 128
X_SIZE = 4


def chain_plan(context_size, x_size, x_first_mask):
    y_bits = [x_size << k for k in range((context_size // x_size).bit_length() - 1)][::-1]
    steps = [(bit, bit) for bit in y_bits]
    if x_size == 4:
        steps += [(1, 1), (3, 2)] if x_first_mask == 1 else [(3, 2), (1, 3)]
    else:
        steps += [(1 << k, 1 << k) for k in range(x_size.bit_length() - 1)]
    return steps


def upper_of(index, mask):
    bits = index & mask
    parity = jnp.zeros_like(index)
    for k in range(mask.bit_length()):
        parity = parity ^ ((bits >> k) & 1)
    return parity != 0


def upper_static(index, mask):
    return bin(index & mask).count("1") % 2 == 1


def stacked_sources(context_size, steps):
    lists = [[c] for c in range(context_size)]
    for mask, side in steps:
        lists = [
            (lists[c ^ mask] + lists[c]) if upper_static(c, side) else (lists[c] + lists[c ^ mask])
            for c in range(context_size)
        ]
    assert all(entry == lists[0] for entry in lists)
    return lists[0]


def exchange_gather(block, steps, axis_name, count):
    index = lax.axis_index(axis_name)
    stack = block
    for mask, side in steps:
        received = lax.ppermute(stack, axis_name, [(i, i ^ mask) for i in range(count)])
        stack = jnp.where(
            upper_of(index, side),
            jnp.concatenate([received, stack], 1),
            jnp.concatenate([stack, received], 1),
        )
    return stack


def unpermute_blocks(product, sources, x_size):
    rows = product.shape[0]
    count = len(sources)
    y_count = count // x_size
    x_order = [sources[ix * y_count] % x_size for ix in range(x_size)]
    y_order = [sources[iy] // x_size for iy in range(y_count)]
    assert all(
        sources[ix * y_count + iy] == y_order[iy] * x_size + x_order[ix]
        for ix in range(x_size)
        for iy in range(y_count)
    )
    product = product.reshape(rows, x_size, y_count, -1)
    x_inverse = [x_order.index(x) for x in range(x_size)]
    y_inverse = [y_order.index(y) for y in range(y_count)]
    if x_inverse != list(range(x_size)):
        product = jnp.concatenate([product[:, i : i + 1] for i in x_inverse], axis=1)
    if y_inverse != list(range(y_count)):
        product = jnp.concatenate([product[:, :, i : i + 1] for i in y_inverse], axis=2)
    return jnp.swapaxes(product, 1, 2).reshape(rows, -1)


def exchange_gather_pair(stack_a, steps_a, stack_b, steps_b, axis_name, count):
    index = lax.axis_index(axis_name)
    for (mask_a, side_a), (mask_b, side_b) in zip(steps_a, steps_b):
        received_a = lax.ppermute(stack_a, axis_name, [(i, i ^ mask_a) for i in range(count)])
        received_b = lax.ppermute(stack_b, axis_name, [(i, i ^ mask_b) for i in range(count)])
        stack_a = jnp.where(
            upper_of(index, side_a),
            jnp.concatenate([received_a, stack_a], 1),
            jnp.concatenate([stack_a, received_a], 1),
        )
        stack_b = jnp.where(
            upper_of(index, side_b),
            jnp.concatenate([received_b, stack_b], 1),
            jnp.concatenate([stack_b, received_b], 1),
        )
        stack_a, stack_b = lax.optimization_barrier((stack_a, stack_b))
    return stack_a, stack_b


def restack(stack, sources, target, x_size):
    rows, count = stack.shape[:2]
    y_count = count // x_size
    x_from = [sources[ix * y_count] for ix in range(x_size)]
    x_to = [target[ix * y_count] for ix in range(x_size)]
    assert all(
        sources[ix * y_count + iy] - x_from[ix] == target[ix * y_count + iy] - x_to[ix]
        for ix in range(x_size)
        for iy in range(y_count)
    )
    picks = [x_from.index(x) for x in x_to]
    if picks == list(range(x_size)):
        return stack
    stack = stack.reshape(rows, x_size, y_count, -1)
    stack = jnp.concatenate([stack[:, i : i + 1] for i in picks], axis=1)
    return stack.reshape(rows, count, -1)


def per_device(queries, keys, values, order, out_weight):
    row_count = queries.shape[0]
    local_groups = keys.shape[1] // HEAD_SIZE
    query_head_group = QUERY_HEADS // KEY_VALUE_HEADS
    score_scale = 1.0 / math.sqrt(HEAD_SIZE)
    context_size = lax.axis_size("context")
    dp_size = lax.axis_size("dp")
    x_size = X_SIZE if context_size % X_SIZE == 0 and context_size > X_SIZE else 1

    core = lax.axis_index("dp") % 2
    weight_rows, weight_cols = out_weight.shape
    half_rows = weight_rows // 2
    quarter = half_rows // 2
    mine = lax.dynamic_slice_in_dim(out_weight, core * half_rows, half_rows, 0)
    steps_a = chain_plan(context_size, x_size, 1)
    steps_b = chain_plan(context_size, x_size, 3)
    shared = 0
    while shared < min(len(steps_a), len(steps_b)) and steps_a[shared] == steps_b[shared]:
        shared += 1
    key_width = keys.shape[1]
    quarters = [
        mine[k * quarter : (k + 1) * quarter].T.reshape(row_count, -1) for k in range(2)
    ]
    block = jnp.concatenate([keys, quarters[0], values, quarters[1]], axis=1)[:, None, :]
    gathered = exchange_gather(block, steps_a[:shared], "context", context_size)
    gathered_a, gathered_b = exchange_gather_pair(
        gathered[:, :, : key_width + weight_cols],
        steps_a[shared:],
        gathered[:, :, key_width + weight_cols :],
        steps_b[shared:],
        "context",
        context_size,
    )
    sources_a = stacked_sources(context_size, steps_a)
    sources_b = stacked_sources(context_size, steps_b)

    mine_weights = jnp.concatenate(
        [gathered_a[:, :, key_width:], gathered_b[:, :, values.shape[1] :]], axis=0
    )
    other_weights = lax.ppermute(mine_weights, "dp", [(i, i ^ 1) for i in range(dp_size)])

    key_stack = gathered_a[:, :, :key_width]
    value_stack = restack(gathered_b[:, :, : values.shape[1]], sources_b, sources_a, x_size)
    key_part = jnp.swapaxes(key_stack, 0, 1).reshape(context_size * row_count, key_width)
    value_part = jnp.swapaxes(value_stack, 0, 1).reshape(context_size * row_count, -1)
    key_pos = order.reshape(context_size, row_count)[jnp.array(sources_a)].reshape(-1)

    first_row = lax.axis_index("context") * row_count
    query_pos = lax.dynamic_slice_in_dim(order, first_row, row_count, 0)
    stacked = queries.reshape(row_count, local_groups, query_head_group, HEAD_SIZE)
    stacked = stacked.transpose(1, 2, 0, 3).reshape(
        local_groups, query_head_group * row_count, HEAD_SIZE
    )
    stacked_pos = jnp.tile(query_pos, query_head_group)
    stacked_rows = query_head_group * row_count
    key_count = key_part.shape[0]
    running_max = jnp.full((local_groups, stacked_rows), -1e30, jnp.float32)
    key_heads = key_part.reshape(key_count, local_groups, HEAD_SIZE)
    value_heads = value_part.reshape(key_count, local_groups, HEAD_SIZE)
    scores = (
        jnp.einsum("grd,kgd->grk", stacked, key_heads, preferred_element_type=jnp.float32)
        * score_scale
    )
    visible = key_pos[None, None, :] <= stacked_pos[None, :, None]
    scores = jnp.where(visible, scores, -1e30)
    new_max = jnp.maximum(running_max, jnp.max(scores, axis=2))
    weights = jnp.where(visible, jnp.exp(scores - new_max[..., None]), 0.0)
    new_sum = jnp.sum(weights, axis=2)
    product = jnp.einsum(
        "grk,kgd->grd",
        weights.astype(jnp.bfloat16),
        value_heads,
        preferred_element_type=jnp.float32,
    )
    attended = (product / new_sum[..., None]).astype(jnp.bfloat16)
    attended = attended.reshape(local_groups, query_head_group, row_count, HEAD_SIZE).transpose(
        2, 0, 1, 3
    )
    attended = attended.reshape(row_count, local_groups * query_head_group * HEAD_SIZE)

    total = None
    for piece, sources in ((0, sources_a), (1, sources_b)):
        for which, held in ((0, mine_weights), (1, other_weights)):
            piece_t = held[piece * row_count : (piece + 1) * row_count]
            piece_t = jnp.swapaxes(piece_t, 0, 1).reshape(context_size, weight_cols, quarter)
            owner = core if which == 0 else 1 - core
            piece_rows = lax.dynamic_slice_in_dim(
                attended, owner * half_rows + piece * quarter, quarter, 1
            )
            product_out = jnp.einsum(
                "rh,nkh->rnk", piece_rows, piece_t, preferred_element_type=jnp.float32
            ).reshape(row_count, -1)
            product_out = unpermute_blocks(product_out, sources, x_size)
            total = product_out if total is None else total + product_out
    partial_out = total
    tensor_size = lax.axis_size("tensor")
    pieces = partial_out.astype(jnp.bfloat16).reshape(row_count, tensor_size, -1)
    pieces = lax.all_to_all(pieces, "tensor", 1, 1, tiled=True)
    return jnp.sum(pieces.astype(jnp.float32), axis=1).astype(jnp.bfloat16)


def solution(mesh):
    placed = (
        P(("dp", "context"), "tensor"),
        P(("dp", "context"), "tensor"),
        P(("dp", "context"), "tensor"),
        P("dp"),
        P("tensor", "context"),
    )
    return jax.shard_map(
        per_device,
        mesh=mesh,
        in_specs=placed,
        out_specs=P(("dp", "context"), "tensor"),
        check_vma=False,
    )
```

```python
import math

import jax
import jax.numpy as jnp
from jax import lax
from jax.sharding import PartitionSpec as P

QUERY_HEADS = 32
KEY_VALUE_HEADS = 8
HEAD_SIZE = 128
X_SIZE = 4


def chain_plan(context_size, x_size, x_first_mask):
    y_bits = [x_size << k for k in range((context_size // x_size).bit_length() - 1)][::-1]
    steps = [(bit, bit) for bit in y_bits]
    if x_size == 4:
        steps += [(1, 1), (3, 2)] if x_first_mask == 1 else [(3, 2), (1, 3)]
    else:
        steps += [(1 << k, 1 << k) for k in range(x_size.bit_length() - 1)]
    return steps


def upper_of(index, mask):
    bits = index & mask
    parity = jnp.zeros_like(index)
    for k in range(mask.bit_length()):
        parity = parity ^ ((bits >> k) & 1)
    return parity != 0


def upper_static(index, mask):
    return bin(index & mask).count("1") % 2 == 1


def stacked_sources(context_size, steps):
    lists = [[c] for c in range(context_size)]
    for mask, side in steps:
        lists = [
            (lists[c ^ mask] + lists[c]) if upper_static(c, side) else (lists[c] + lists[c ^ mask])
            for c in range(context_size)
        ]
    assert all(entry == lists[0] for entry in lists)
    return lists[0]


def exchange_gather(block, steps, axis_name, count):
    index = lax.axis_index(axis_name)
    stack = block
    for mask, side in steps:
        received = lax.ppermute(stack, axis_name, [(i, i ^ mask) for i in range(count)])
        stack = jnp.where(
            upper_of(index, side),
            jnp.concatenate([received, stack], 1),
            jnp.concatenate([stack, received], 1),
        )
    return stack


def unpermute_blocks(product, sources, x_size):
    rows = product.shape[0]
    count = len(sources)
    y_count = count // x_size
    x_order = [sources[ix * y_count] % x_size for ix in range(x_size)]
    y_order = [sources[iy] // x_size for iy in range(y_count)]
    assert all(
        sources[ix * y_count + iy] == y_order[iy] * x_size + x_order[ix]
        for ix in range(x_size)
        for iy in range(y_count)
    )
    product = product.reshape(rows, x_size, y_count, -1)
    x_inverse = [x_order.index(x) for x in range(x_size)]
    y_inverse = [y_order.index(y) for y in range(y_count)]
    if x_inverse != list(range(x_size)):
        product = jnp.concatenate([product[:, i : i + 1] for i in x_inverse], axis=1)
    if y_inverse != list(range(y_count)):
        product = jnp.concatenate([product[:, :, i : i + 1] for i in y_inverse], axis=2)
    return jnp.swapaxes(product, 1, 2).reshape(rows, -1)


def exchange_gather_pair(stack_a, steps_a, stack_b, steps_b, axis_name, count):
    index = lax.axis_index(axis_name)
    for (mask_a, side_a), (mask_b, side_b) in zip(steps_a, steps_b):
        received_a = lax.ppermute(stack_a, axis_name, [(i, i ^ mask_a) for i in range(count)])
        received_b = lax.ppermute(stack_b, axis_name, [(i, i ^ mask_b) for i in range(count)])
        stack_a = jnp.where(
            upper_of(index, side_a),
            jnp.concatenate([received_a, stack_a], 1),
            jnp.concatenate([stack_a, received_a], 1),
        )
        stack_b = jnp.where(
            upper_of(index, side_b),
            jnp.concatenate([received_b, stack_b], 1),
            jnp.concatenate([stack_b, received_b], 1),
        )
        stack_a, stack_b = lax.optimization_barrier((stack_a, stack_b))
    return stack_a, stack_b


def restack(stack, sources, target, x_size):
    rows, count = stack.shape[:2]
    y_count = count // x_size
    x_from = [sources[ix * y_count] for ix in range(x_size)]
    x_to = [target[ix * y_count] for ix in range(x_size)]
    assert all(
        sources[ix * y_count + iy] - x_from[ix] == target[ix * y_count + iy] - x_to[ix]
        for ix in range(x_size)
        for iy in range(y_count)
    )
    picks = [x_from.index(x) for x in x_to]
    if picks == list(range(x_size)):
        return stack
    stack = stack.reshape(rows, x_size, y_count, -1)
    stack = jnp.concatenate([stack[:, i : i + 1] for i in picks], axis=1)
    return stack.reshape(rows, count, -1)


def per_device(queries, keys, values, order, out_weight):
    row_count = queries.shape[0]
    local_groups = keys.shape[1] // HEAD_SIZE
    query_head_group = QUERY_HEADS // KEY_VALUE_HEADS
    score_scale = 1.0 / math.sqrt(HEAD_SIZE)
    context_size = lax.axis_size("context")
    dp_size = lax.axis_size("dp")
    x_size = X_SIZE if context_size % X_SIZE == 0 and context_size > X_SIZE else 1

    core = lax.axis_index("dp") % 2
    weight_rows, weight_cols = out_weight.shape
    half_rows = weight_rows // 2
    quarter = half_rows // 2
    mine = lax.dynamic_slice_in_dim(out_weight, core * half_rows, half_rows, 0)
    steps_a = chain_plan(context_size, x_size, 1)
    steps_b = chain_plan(context_size, x_size, 3)
    shared = 0
    while shared < min(len(steps_a), len(steps_b)) and steps_a[shared] == steps_b[shared]:
        shared += 1
    key_width = keys.shape[1]
    quarters = [
        mine[k * quarter : (k + 1) * quarter].T.reshape(row_count, -1) for k in range(2)
    ]
    block = jnp.concatenate([keys, quarters[0], values, quarters[1]], axis=1)[:, None, :]
    gathered = exchange_gather(block, steps_a[:shared], "context", context_size)
    gathered_a, gathered_b = exchange_gather_pair(
        gathered[:, :, : key_width + weight_cols],
        steps_a[shared:],
        gathered[:, :, key_width + weight_cols :],
        steps_b[shared:],
        "context",
        context_size,
    )
    sources_a = stacked_sources(context_size, steps_a)
    sources_b = stacked_sources(context_size, steps_b)

    mine_weights = jnp.concatenate(
        [gathered_a[:, :, key_width:], gathered_b[:, :, values.shape[1] :]], axis=0
    )
    other_weights = lax.ppermute(mine_weights, "dp", [(i, i ^ 1) for i in range(dp_size)])

    key_stack = gathered_a[:, :, :key_width]
    value_stack = restack(gathered_b[:, :, : values.shape[1]], sources_b, sources_a, x_size)
    key_part = jnp.swapaxes(key_stack, 0, 1).reshape(context_size * row_count, key_width)
    value_part = jnp.swapaxes(value_stack, 0, 1).reshape(context_size * row_count, -1)
    key_pos = order.reshape(context_size, row_count)[jnp.array(sources_a)].reshape(-1)

    first_row = lax.axis_index("context") * row_count
    query_pos = lax.dynamic_slice_in_dim(order, first_row, row_count, 0)
    stacked = queries.reshape(row_count, local_groups, query_head_group, HEAD_SIZE)
    stacked = stacked.transpose(1, 2, 0, 3).reshape(
        local_groups, query_head_group * row_count, HEAD_SIZE
    )
    stacked_pos = jnp.tile(query_pos, query_head_group)
    stacked_rows = query_head_group * row_count
    key_count = key_part.shape[0]
    running_max = jnp.full((local_groups, stacked_rows), -1e30, jnp.float32)
    key_heads = key_part.reshape(key_count, local_groups, HEAD_SIZE)
    value_heads = value_part.reshape(key_count, local_groups, HEAD_SIZE)
    scores = (
        jnp.einsum("grd,kgd->grk", stacked, key_heads, preferred_element_type=jnp.float32)
        * score_scale
    )
    visible = key_pos[None, None, :] <= stacked_pos[None, :, None]
    scores = jnp.where(visible, scores, -1e30)
    new_max = jnp.maximum(running_max, jnp.max(scores, axis=2))
    weights = jnp.where(visible, jnp.exp(scores - new_max[..., None]), 0.0)
    new_sum = jnp.sum(weights, axis=2)
    product = jnp.einsum(
        "grk,kgd->grd",
        weights.astype(jnp.bfloat16),
        value_heads,
        preferred_element_type=jnp.float32,
    )
    attended = (product / new_sum[..., None]).astype(jnp.bfloat16)
    attended = attended.reshape(local_groups, query_head_group, row_count, HEAD_SIZE).transpose(
        2, 0, 1, 3
    )
    attended = attended.reshape(row_count, local_groups * query_head_group * HEAD_SIZE)

    total = None
    for piece, sources in ((0, sources_a), (1, sources_b)):
        piece_sum = None
        for which, held in ((0, mine_weights), (1, other_weights)):
            piece_t = held[piece * row_count : (piece + 1) * row_count]
            piece_t = jnp.swapaxes(piece_t, 0, 1).reshape(context_size, weight_cols, quarter)
            owner = core if which == 0 else 1 - core
            piece_rows = lax.dynamic_slice_in_dim(
                attended, owner * half_rows + piece * quarter, quarter, 1
            )
            product_out = jnp.einsum(
                "rh,nkh->rnk", piece_rows, piece_t, preferred_element_type=jnp.float32
            ).reshape(row_count, -1)
            piece_sum = product_out if piece_sum is None else piece_sum + product_out
        piece_sum = unpermute_blocks(piece_sum, sources, x_size)
        total = piece_sum if total is None else total + piece_sum
    partial_out = total
    tensor_size = lax.axis_size("tensor")
    pieces = partial_out.astype(jnp.bfloat16).reshape(row_count, tensor_size, -1)
    pieces = lax.all_to_all(pieces, "tensor", 1, 1, tiled=True)
    return jnp.sum(pieces.astype(jnp.float32), axis=1).astype(jnp.bfloat16)


def solution(mesh):
    placed = (
        P(("dp", "context"), "tensor"),
        P(("dp", "context"), "tensor"),
        P(("dp", "context"), "tensor"),
        P("dp"),
        P("tensor", "context"),
    )
    return jax.shard_map(
        per_device,
        mesh=mesh,
        in_specs=placed,
        out_specs=P(("dp", "context"), "tensor"),
        check_vma=False,
    )
```

```python
import math

import jax
import jax.numpy as jnp
from jax import lax
from jax.sharding import PartitionSpec as P

QUERY_HEADS = 32
KEY_VALUE_HEADS = 8
HEAD_SIZE = 128
X_SIZE = 4


def chain_plan(context_size, x_size, x_first_mask):
    y_bits = [x_size << k for k in range((context_size // x_size).bit_length() - 1)][::-1]
    steps = [(bit, bit) for bit in y_bits]
    if x_size == 4:
        steps += [(1, 1), (3, 2)] if x_first_mask == 1 else [(3, 2), (1, 3)]
    else:
        steps += [(1 << k, 1 << k) for k in range(x_size.bit_length() - 1)]
    return steps


def upper_of(index, mask):
    bits = index & mask
    parity = jnp.zeros_like(index)
    for k in range(mask.bit_length()):
        parity = parity ^ ((bits >> k) & 1)
    return parity != 0


def upper_static(index, mask):
    return bin(index & mask).count("1") % 2 == 1


def stacked_sources(context_size, steps):
    lists = [[c] for c in range(context_size)]
    for mask, side in steps:
        lists = [
            (lists[c ^ mask] + lists[c]) if upper_static(c, side) else (lists[c] + lists[c ^ mask])
            for c in range(context_size)
        ]
    assert all(entry == lists[0] for entry in lists)
    return lists[0]


def exchange_gather(block, steps, axis_name, count):
    index = lax.axis_index(axis_name)
    stack = block
    for mask, side in steps:
        received = lax.ppermute(stack, axis_name, [(i, i ^ mask) for i in range(count)])
        stack = jnp.where(
            upper_of(index, side),
            jnp.concatenate([received, stack], 1),
            jnp.concatenate([stack, received], 1),
        )
    return stack


def unpermute_blocks(product, sources, x_size):
    rows = product.shape[0]
    count = len(sources)
    y_count = count // x_size
    x_order = [sources[ix * y_count] % x_size for ix in range(x_size)]
    y_order = [sources[iy] // x_size for iy in range(y_count)]
    assert all(
        sources[ix * y_count + iy] == y_order[iy] * x_size + x_order[ix]
        for ix in range(x_size)
        for iy in range(y_count)
    )
    product = product.reshape(rows, x_size, y_count, -1)
    x_inverse = [x_order.index(x) for x in range(x_size)]
    y_inverse = [y_order.index(y) for y in range(y_count)]
    if x_inverse != list(range(x_size)):
        product = jnp.concatenate([product[:, i : i + 1] for i in x_inverse], axis=1)
    if y_inverse != list(range(y_count)):
        product = jnp.concatenate([product[:, :, i : i + 1] for i in y_inverse], axis=2)
    return jnp.swapaxes(product, 1, 2).reshape(rows, -1)


def exchange_gather_pair(stack_a, steps_a, stack_b, steps_b, axis_name, count):
    index = lax.axis_index(axis_name)
    for (mask_a, side_a), (mask_b, side_b) in zip(steps_a, steps_b):
        received_a = lax.ppermute(stack_a, axis_name, [(i, i ^ mask_a) for i in range(count)])
        received_b = lax.ppermute(stack_b, axis_name, [(i, i ^ mask_b) for i in range(count)])
        stack_a = jnp.where(
            upper_of(index, side_a),
            jnp.concatenate([received_a, stack_a], 1),
            jnp.concatenate([stack_a, received_a], 1),
        )
        stack_b = jnp.where(
            upper_of(index, side_b),
            jnp.concatenate([received_b, stack_b], 1),
            jnp.concatenate([stack_b, received_b], 1),
        )
        stack_a, stack_b = lax.optimization_barrier((stack_a, stack_b))
    return stack_a, stack_b


def restack(stack, sources, target, x_size):
    rows, count = stack.shape[:2]
    y_count = count // x_size
    x_from = [sources[ix * y_count] for ix in range(x_size)]
    x_to = [target[ix * y_count] for ix in range(x_size)]
    assert all(
        sources[ix * y_count + iy] - x_from[ix] == target[ix * y_count + iy] - x_to[ix]
        for ix in range(x_size)
        for iy in range(y_count)
    )
    picks = [x_from.index(x) for x in x_to]
    if picks == list(range(x_size)):
        return stack
    stack = stack.reshape(rows, x_size, y_count, -1)
    stack = jnp.concatenate([stack[:, i : i + 1] for i in picks], axis=1)
    return stack.reshape(rows, count, -1)


def per_device(queries, keys, values, order, out_weight):
    row_count = queries.shape[0]
    local_groups = keys.shape[1] // HEAD_SIZE
    query_head_group = QUERY_HEADS // KEY_VALUE_HEADS
    score_scale = 1.0 / math.sqrt(HEAD_SIZE)
    context_size = lax.axis_size("context")
    dp_size = lax.axis_size("dp")
    x_size = X_SIZE if context_size % X_SIZE == 0 and context_size > X_SIZE else 1

    core = lax.axis_index("dp") % 2
    weight_rows, weight_cols = out_weight.shape
    half_rows = weight_rows // 2
    quarter = half_rows // 2
    mine = lax.dynamic_slice_in_dim(out_weight, core * half_rows, half_rows, 0)
    steps_a = chain_plan(context_size, x_size, 1)
    steps_b = chain_plan(context_size, x_size, 3)
    shared = 0
    while shared < min(len(steps_a), len(steps_b)) and steps_a[shared] == steps_b[shared]:
        shared += 1
    key_width = keys.shape[1]
    quarters = [
        mine[k * quarter : (k + 1) * quarter].T.reshape(row_count, -1) for k in range(2)
    ]
    block = jnp.concatenate([keys, quarters[0], values, quarters[1]], axis=1)[:, None, :]
    gathered = exchange_gather(block, steps_a[:shared], "context", context_size)
    gathered_a, gathered_b = exchange_gather_pair(
        gathered[:, :, : key_width + weight_cols],
        steps_a[shared:],
        gathered[:, :, key_width + weight_cols :],
        steps_b[shared:],
        "context",
        context_size,
    )
    sources_a = stacked_sources(context_size, steps_a)
    sources_b = stacked_sources(context_size, steps_b)

    other_a, other_b = lax.ppermute(
        (gathered_a, gathered_b), "dp", [(i, i ^ 1) for i in range(dp_size)]
    )
    mine_weights = (gathered_a[:, :, key_width:], gathered_b[:, :, values.shape[1] :])
    other_weights = (other_a[:, :, key_width:], other_b[:, :, values.shape[1] :])

    key_stack = gathered_a[:, :, :key_width]
    value_stack = restack(gathered_b[:, :, : values.shape[1]], sources_b, sources_a, x_size)
    key_part = jnp.swapaxes(key_stack, 0, 1).reshape(context_size * row_count, key_width)
    value_part = jnp.swapaxes(value_stack, 0, 1).reshape(context_size * row_count, -1)
    key_pos = order.reshape(context_size, row_count)[jnp.array(sources_a)].reshape(-1)

    first_row = lax.axis_index("context") * row_count
    query_pos = lax.dynamic_slice_in_dim(order, first_row, row_count, 0)
    stacked = queries.reshape(row_count, local_groups, query_head_group, HEAD_SIZE)
    stacked = stacked.transpose(1, 2, 0, 3).reshape(
        local_groups, query_head_group * row_count, HEAD_SIZE
    )
    stacked_pos = jnp.tile(query_pos, query_head_group)
    stacked_rows = query_head_group * row_count
    key_count = key_part.shape[0]
    running_max = jnp.full((local_groups, stacked_rows), -1e30, jnp.float32)
    key_heads = key_part.reshape(key_count, local_groups, HEAD_SIZE)
    value_heads = value_part.reshape(key_count, local_groups, HEAD_SIZE)
    scores = (
        jnp.einsum("grd,kgd->grk", stacked, key_heads, preferred_element_type=jnp.float32)
        * score_scale
    )
    visible = key_pos[None, None, :] <= stacked_pos[None, :, None]
    scores = jnp.where(visible, scores, -1e30)
    new_max = jnp.maximum(running_max, jnp.max(scores, axis=2))
    weights = jnp.where(visible, jnp.exp(scores - new_max[..., None]), 0.0)
    new_sum = jnp.sum(weights, axis=2)
    product = jnp.einsum(
        "grk,kgd->grd",
        weights.astype(jnp.bfloat16),
        value_heads,
        preferred_element_type=jnp.float32,
    )
    attended = (product / new_sum[..., None]).astype(jnp.bfloat16)
    attended = attended.reshape(local_groups, query_head_group, row_count, HEAD_SIZE).transpose(
        2, 0, 1, 3
    )
    attended = attended.reshape(row_count, local_groups * query_head_group * HEAD_SIZE)

    total = None
    for piece, sources in ((0, sources_a), (1, sources_b)):
        for which, held in ((0, mine_weights), (1, other_weights)):
            piece_t = held[piece]
            piece_t = jnp.swapaxes(piece_t, 0, 1).reshape(context_size, weight_cols, quarter)
            owner = core if which == 0 else 1 - core
            piece_rows = lax.dynamic_slice_in_dim(
                attended, owner * half_rows + piece * quarter, quarter, 1
            )
            product_out = jnp.einsum(
                "rh,nkh->rnk", piece_rows, piece_t, preferred_element_type=jnp.float32
            ).reshape(row_count, -1)
            product_out = unpermute_blocks(product_out, sources, x_size)
            total = product_out if total is None else total + product_out
    partial_out = total
    tensor_size = lax.axis_size("tensor")
    pieces = partial_out.astype(jnp.bfloat16).reshape(row_count, tensor_size, -1)
    pieces = lax.all_to_all(pieces, "tensor", 1, 1, tiled=True)
    return jnp.sum(pieces.astype(jnp.float32), axis=1).astype(jnp.bfloat16)


def solution(mesh):
    placed = (
        P(("dp", "context"), "tensor"),
        P(("dp", "context"), "tensor"),
        P(("dp", "context"), "tensor"),
        P("dp"),
        P("tensor", "context"),
    )
    return jax.shard_map(
        per_device,
        mesh=mesh,
        in_specs=placed,
        out_specs=P(("dp", "context"), "tensor"),
        check_vma=False,
    )
```

```python
import math

import jax
import jax.numpy as jnp
from jax import lax
from jax.sharding import PartitionSpec as P

QUERY_HEADS = 32
KEY_VALUE_HEADS = 8
HEAD_SIZE = 128
X_SIZE = 4


def chain_plan(context_size, x_size, x_first_mask):
    y_bits = [x_size << k for k in range((context_size // x_size).bit_length() - 1)][::-1]
    steps = [(bit, bit) for bit in y_bits]
    if x_size == 4:
        steps += [(1, 1), (3, 2)] if x_first_mask == 1 else [(3, 2), (1, 3)]
    else:
        steps += [(1 << k, 1 << k) for k in range(x_size.bit_length() - 1)]
    return steps


def upper_of(index, mask):
    bits = index & mask
    parity = jnp.zeros_like(index)
    for k in range(mask.bit_length()):
        parity = parity ^ ((bits >> k) & 1)
    return parity != 0


def upper_static(index, mask):
    return bin(index & mask).count("1") % 2 == 1


def stacked_sources(context_size, steps):
    lists = [[c] for c in range(context_size)]
    for mask, side in steps:
        lists = [
            (lists[c ^ mask] + lists[c]) if upper_static(c, side) else (lists[c] + lists[c ^ mask])
            for c in range(context_size)
        ]
    assert all(entry == lists[0] for entry in lists)
    return lists[0]


def exchange_gather(block, steps, axis_name, count):
    index = lax.axis_index(axis_name)
    stack = block
    for mask, side in steps:
        received = lax.ppermute(stack, axis_name, [(i, i ^ mask) for i in range(count)])
        stack = jnp.where(
            upper_of(index, side),
            jnp.concatenate([received, stack], 1),
            jnp.concatenate([stack, received], 1),
        )
    return stack


def unpermute_blocks(product, sources, x_size):
    rows = product.shape[0]
    count = len(sources)
    y_count = count // x_size
    x_order = [sources[ix * y_count] % x_size for ix in range(x_size)]
    y_order = [sources[iy] // x_size for iy in range(y_count)]
    assert all(
        sources[ix * y_count + iy] == y_order[iy] * x_size + x_order[ix]
        for ix in range(x_size)
        for iy in range(y_count)
    )
    product = product.reshape(rows, x_size, y_count, -1)
    x_inverse = [x_order.index(x) for x in range(x_size)]
    y_inverse = [y_order.index(y) for y in range(y_count)]
    if x_inverse != list(range(x_size)):
        product = jnp.concatenate([product[:, i : i + 1] for i in x_inverse], axis=1)
    if y_inverse != list(range(y_count)):
        product = jnp.concatenate([product[:, :, i : i + 1] for i in y_inverse], axis=2)
    return jnp.swapaxes(product, 1, 2).reshape(rows, -1)


def exchange_gather_pair(stack_a, steps_a, stack_b, steps_b, axis_name, count):
    index = lax.axis_index(axis_name)
    for (mask_a, side_a), (mask_b, side_b) in zip(steps_a, steps_b):
        received_a = lax.ppermute(stack_a, axis_name, [(i, i ^ mask_a) for i in range(count)])
        received_b = lax.ppermute(stack_b, axis_name, [(i, i ^ mask_b) for i in range(count)])
        stack_a = jnp.where(
            upper_of(index, side_a),
            jnp.concatenate([received_a, stack_a], 1),
            jnp.concatenate([stack_a, received_a], 1),
        )
        stack_b = jnp.where(
            upper_of(index, side_b),
            jnp.concatenate([received_b, stack_b], 1),
            jnp.concatenate([stack_b, received_b], 1),
        )
        stack_a, stack_b = lax.optimization_barrier((stack_a, stack_b))
    return stack_a, stack_b


def restack(stack, sources, target, x_size):
    rows, count = stack.shape[:2]
    y_count = count // x_size
    x_from = [sources[ix * y_count] for ix in range(x_size)]
    x_to = [target[ix * y_count] for ix in range(x_size)]
    assert all(
        sources[ix * y_count + iy] - x_from[ix] == target[ix * y_count + iy] - x_to[ix]
        for ix in range(x_size)
        for iy in range(y_count)
    )
    picks = [x_from.index(x) for x in x_to]
    if picks == list(range(x_size)):
        return stack
    stack = stack.reshape(rows, x_size, y_count, -1)
    stack = jnp.concatenate([stack[:, i : i + 1] for i in picks], axis=1)
    return stack.reshape(rows, count, -1)


def per_device(queries, keys, values, order, out_weight):
    row_count = queries.shape[0]
    local_groups = keys.shape[1] // HEAD_SIZE
    query_head_group = QUERY_HEADS // KEY_VALUE_HEADS
    score_scale = 1.0 / math.sqrt(HEAD_SIZE)
    context_size = lax.axis_size("context")
    dp_size = lax.axis_size("dp")
    x_size = X_SIZE if context_size % X_SIZE == 0 and context_size > X_SIZE else 1

    core = lax.axis_index("dp") % 2
    weight_rows, weight_cols = out_weight.shape
    half_rows = weight_rows // 2
    quarter = half_rows // 2
    mine = lax.dynamic_slice_in_dim(out_weight, core * half_rows, half_rows, 0)
    steps_a = chain_plan(context_size, x_size, 1)
    steps_b = chain_plan(context_size, x_size, 3)
    shared = 0
    while shared < min(len(steps_a), len(steps_b)) and steps_a[shared] == steps_b[shared]:
        shared += 1
    key_width = keys.shape[1]
    assert keys.shape[1] == quarter and values.shape[1] == quarter
    block_a = jnp.concatenate([keys, mine[:quarter].T], axis=0)[:, None, :]
    block_b = jnp.concatenate([values, mine[quarter:].T], axis=0)[:, None, :]
    block = jnp.concatenate([block_a, block_b], axis=2)
    gathered = exchange_gather(block, steps_a[:shared], "context", context_size)
    gathered_a, gathered_b = exchange_gather_pair(
        gathered[:, :, :quarter],
        steps_a[shared:],
        gathered[:, :, quarter:],
        steps_b[shared:],
        "context",
        context_size,
    )
    sources_a = stacked_sources(context_size, steps_a)
    sources_b = stacked_sources(context_size, steps_b)

    other_a, other_b = lax.ppermute(
        (gathered_a, gathered_b), "dp", [(i, i ^ 1) for i in range(dp_size)]
    )
    mine_weights = (gathered_a, gathered_b)
    other_weights = (other_a, other_b)

    key_stack = gathered_a[:row_count]
    value_stack = restack(gathered_b[:row_count], sources_b, sources_a, x_size)
    key_part = jnp.swapaxes(key_stack, 0, 1).reshape(context_size * row_count, key_width)
    value_part = jnp.swapaxes(value_stack, 0, 1).reshape(context_size * row_count, -1)
    key_pos = order.reshape(context_size, row_count)[jnp.array(sources_a)].reshape(-1)

    first_row = lax.axis_index("context") * row_count
    query_pos = lax.dynamic_slice_in_dim(order, first_row, row_count, 0)
    stacked = queries.reshape(row_count, local_groups, query_head_group, HEAD_SIZE)
    stacked = stacked.transpose(1, 2, 0, 3).reshape(
        local_groups, query_head_group * row_count, HEAD_SIZE
    )
    stacked_pos = jnp.tile(query_pos, query_head_group)
    stacked_rows = query_head_group * row_count
    key_count = key_part.shape[0]
    running_max = jnp.full((local_groups, stacked_rows), -1e30, jnp.float32)
    key_heads = key_part.reshape(key_count, local_groups, HEAD_SIZE)
    value_heads = value_part.reshape(key_count, local_groups, HEAD_SIZE)
    scores = (
        jnp.einsum("grd,kgd->grk", stacked, key_heads, preferred_element_type=jnp.float32)
        * score_scale
    )
    visible = key_pos[None, None, :] <= stacked_pos[None, :, None]
    scores = jnp.where(visible, scores, -1e30)
    new_max = jnp.maximum(running_max, jnp.max(scores, axis=2))
    weights = jnp.where(visible, jnp.exp(scores - new_max[..., None]), 0.0)
    new_sum = jnp.sum(weights, axis=2)
    product = jnp.einsum(
        "grk,kgd->grd",
        weights.astype(jnp.bfloat16),
        value_heads,
        preferred_element_type=jnp.float32,
    )
    attended = (product / new_sum[..., None]).astype(jnp.bfloat16)
    attended = attended.reshape(local_groups, query_head_group, row_count, HEAD_SIZE).transpose(
        2, 0, 1, 3
    )
    attended = attended.reshape(row_count, local_groups * query_head_group * HEAD_SIZE)

    total = None
    for piece, sources in ((0, sources_a), (1, sources_b)):
        for which, held in ((0, mine_weights), (1, other_weights)):
            piece_t = jnp.swapaxes(held[piece], 0, 1)
            owner = core if which == 0 else 1 - core
            piece_rows = lax.dynamic_slice_in_dim(
                attended, owner * half_rows + piece * quarter, quarter, 1
            )
            product_out = jnp.einsum(
                "rh,nkh->rnk", piece_rows, piece_t, preferred_element_type=jnp.float32
            )[:, :, row_count:].reshape(row_count, -1)
            product_out = unpermute_blocks(product_out, sources, x_size)
            total = product_out if total is None else total + product_out
    partial_out = total
    tensor_size = lax.axis_size("tensor")
    pieces = partial_out.astype(jnp.bfloat16).reshape(row_count, tensor_size, -1)
    pieces = lax.all_to_all(pieces, "tensor", 1, 1, tiled=True)
    return jnp.sum(pieces.astype(jnp.float32), axis=1).astype(jnp.bfloat16)


def solution(mesh):
    placed = (
        P(("dp", "context"), "tensor"),
        P(("dp", "context"), "tensor"),
        P(("dp", "context"), "tensor"),
        P("dp"),
        P("tensor", "context"),
    )
    return jax.shard_map(
        per_device,
        mesh=mesh,
        in_specs=placed,
        out_specs=P(("dp", "context"), "tensor"),
        check_vma=False,
    )
```

```python
import math

import jax
import jax.numpy as jnp
from jax import lax
from jax.sharding import PartitionSpec as P

QUERY_HEADS = 32
KEY_VALUE_HEADS = 8
HEAD_SIZE = 128
X_SIZE = 4


def chain_plan(context_size, x_size, x_first_mask):
    y_bits = [x_size << k for k in range((context_size // x_size).bit_length() - 1)][::-1]
    steps = [(bit, bit) for bit in y_bits]
    if x_size == 4:
        steps += [(1, 1), (3, 2)] if x_first_mask == 1 else [(3, 2), (1, 3)]
    else:
        steps += [(1 << k, 1 << k) for k in range(x_size.bit_length() - 1)]
    return steps


def upper_of(index, mask):
    bits = index & mask
    parity = jnp.zeros_like(index)
    for k in range(mask.bit_length()):
        parity = parity ^ ((bits >> k) & 1)
    return parity != 0


def upper_static(index, mask):
    return bin(index & mask).count("1") % 2 == 1


def stacked_sources(context_size, steps):
    lists = [[c] for c in range(context_size)]
    for mask, side in steps:
        lists = [
            (lists[c ^ mask] + lists[c]) if upper_static(c, side) else (lists[c] + lists[c ^ mask])
            for c in range(context_size)
        ]
    assert all(entry == lists[0] for entry in lists)
    return lists[0]


def exchange_gather(block, steps, axis_name, count):
    index = lax.axis_index(axis_name)
    stack = block
    for mask, side in steps:
        received = lax.ppermute(stack, axis_name, [(i, i ^ mask) for i in range(count)])
        stack = jnp.where(
            upper_of(index, side),
            jnp.concatenate([received, stack], 1),
            jnp.concatenate([stack, received], 1),
        )
    return stack


def unpermute_blocks(product, sources, x_size):
    rows = product.shape[0]
    count = len(sources)
    y_count = count // x_size
    x_order = [sources[ix * y_count] % x_size for ix in range(x_size)]
    y_order = [sources[iy] // x_size for iy in range(y_count)]
    assert all(
        sources[ix * y_count + iy] == y_order[iy] * x_size + x_order[ix]
        for ix in range(x_size)
        for iy in range(y_count)
    )
    product = product.reshape(rows, x_size, y_count, -1)
    x_inverse = [x_order.index(x) for x in range(x_size)]
    y_inverse = [y_order.index(y) for y in range(y_count)]
    if x_inverse != list(range(x_size)):
        product = jnp.concatenate([product[:, i : i + 1] for i in x_inverse], axis=1)
    if y_inverse != list(range(y_count)):
        product = jnp.concatenate([product[:, :, i : i + 1] for i in y_inverse], axis=2)
    return jnp.swapaxes(product, 1, 2).reshape(rows, -1)


def exchange_gather_pair(stack_a, steps_a, stack_b, steps_b, axis_name, count):
    index = lax.axis_index(axis_name)
    for (mask_a, side_a), (mask_b, side_b) in zip(steps_a, steps_b):
        received_a = lax.ppermute(stack_a, axis_name, [(i, i ^ mask_a) for i in range(count)])
        received_b = lax.ppermute(stack_b, axis_name, [(i, i ^ mask_b) for i in range(count)])
        stack_a = jnp.where(
            upper_of(index, side_a),
            jnp.concatenate([received_a, stack_a], 1),
            jnp.concatenate([stack_a, received_a], 1),
        )
        stack_b = jnp.where(
            upper_of(index, side_b),
            jnp.concatenate([received_b, stack_b], 1),
            jnp.concatenate([stack_b, received_b], 1),
        )
        stack_a, stack_b = lax.optimization_barrier((stack_a, stack_b))
    return stack_a, stack_b


def restack(stack, sources, target, x_size):
    rows, count = stack.shape[:2]
    y_count = count // x_size
    x_from = [sources[ix * y_count] for ix in range(x_size)]
    x_to = [target[ix * y_count] for ix in range(x_size)]
    assert all(
        sources[ix * y_count + iy] - x_from[ix] == target[ix * y_count + iy] - x_to[ix]
        for ix in range(x_size)
        for iy in range(y_count)
    )
    picks = [x_from.index(x) for x in x_to]
    if picks == list(range(x_size)):
        return stack
    stack = stack.reshape(rows, x_size, y_count, -1)
    stack = jnp.concatenate([stack[:, i : i + 1] for i in picks], axis=1)
    return stack.reshape(rows, count, -1)


def context_order(stack, sources, x_size):
    rows, count = stack.shape[:2]
    y_count = count // x_size
    tail = stack.shape[2:]
    x_major = all(
        sources[ix * y_count + iy]
        == (sources[iy] // x_size) * x_size + sources[ix * y_count] % x_size
        for ix in range(x_size)
        for iy in range(y_count)
    )
    if x_major:
        outer = [sources[ix * y_count] % x_size for ix in range(x_size)]
        inner = [sources[iy] // x_size for iy in range(y_count)]
        shape = (rows, x_size, y_count) + tail
    else:
        outer = [sources[iy * x_size] // x_size for iy in range(y_count)]
        inner = [sources[ix] % x_size for ix in range(x_size)]
        assert all(
            sources[iy * x_size + ix] == outer[iy] * x_size + inner[ix]
            for iy in range(y_count)
            for ix in range(x_size)
        )
        shape = (rows, y_count, x_size) + tail
    stack = stack.reshape(shape)
    outer_pick = [outer.index(v) for v in range(len(outer))]
    inner_pick = [inner.index(v) for v in range(len(inner))]
    if outer_pick != list(range(len(outer))):
        stack = jnp.concatenate([stack[:, i : i + 1] for i in outer_pick], axis=1)
    if inner_pick != list(range(len(inner))):
        stack = jnp.concatenate([stack[:, :, i : i + 1] for i in inner_pick], axis=2)
    if x_major:
        stack = jnp.swapaxes(stack, 1, 2)
    return stack.reshape((rows, count) + tail)


def per_device(queries, keys, values, order, out_weight):
    row_count = queries.shape[0]
    local_groups = keys.shape[1] // HEAD_SIZE
    query_head_group = QUERY_HEADS // KEY_VALUE_HEADS
    score_scale = 1.0 / math.sqrt(HEAD_SIZE)
    context_size = lax.axis_size("context")
    dp_size = lax.axis_size("dp")
    x_size = X_SIZE if context_size % X_SIZE == 0 and context_size > X_SIZE else 1

    core = lax.axis_index("dp") % 2
    weight_rows, weight_cols = out_weight.shape
    half_rows = weight_rows // 2
    quarter = half_rows // 2
    mine = lax.dynamic_slice_in_dim(out_weight, core * half_rows, half_rows, 0)
    steps_a = chain_plan(context_size, x_size, 1)
    steps_b = chain_plan(context_size, x_size, 3)
    if x_size > 1:
        y_steps = len(steps_b) - 2
        steps_b = steps_b[y_steps:] + steps_b[:y_steps]
    quarters = [
        mine[k * quarter : (k + 1) * quarter].T.reshape(row_count, -1) for k in range(2)
    ]
    key_width = keys.shape[1]
    gathered_a, gathered_b = exchange_gather_pair(
        jnp.concatenate([keys, quarters[0]], axis=1)[:, None, :],
        steps_a,
        jnp.concatenate([values, quarters[1]], axis=1)[:, None, :],
        steps_b,
        "context",
        context_size,
    )
    sources_a = stacked_sources(context_size, steps_a)
    sources_b = stacked_sources(context_size, steps_b)

    mine_weights = jnp.concatenate(
        [gathered_a[:, :, key_width:], gathered_b[:, :, values.shape[1] :]], axis=0
    )
    other_weights = lax.ppermute(mine_weights, "dp", [(i, i ^ 1) for i in range(dp_size)])

    key_stack = context_order(gathered_a[:, :, :key_width], sources_a, x_size)
    value_stack = context_order(gathered_b[:, :, : values.shape[1]], sources_b, x_size)
    key_part = jnp.swapaxes(key_stack, 0, 1).reshape(context_size * row_count, key_width)
    value_part = jnp.swapaxes(value_stack, 0, 1).reshape(context_size * row_count, -1)
    key_pos = order

    first_row = lax.axis_index("context") * row_count
    query_pos = lax.dynamic_slice_in_dim(order, first_row, row_count, 0)
    stacked = queries.reshape(row_count, local_groups, query_head_group, HEAD_SIZE)
    stacked = stacked.transpose(1, 2, 0, 3).reshape(
        local_groups, query_head_group * row_count, HEAD_SIZE
    )
    stacked_pos = jnp.tile(query_pos, query_head_group)
    stacked_rows = query_head_group * row_count
    key_count = key_part.shape[0]
    running_max = jnp.full((local_groups, stacked_rows), -1e30, jnp.float32)
    key_heads = key_part.reshape(key_count, local_groups, HEAD_SIZE)
    value_heads = value_part.reshape(key_count, local_groups, HEAD_SIZE)
    scores = (
        jnp.einsum("grd,kgd->grk", stacked, key_heads, preferred_element_type=jnp.float32)
        * score_scale
    )
    visible = key_pos[None, None, :] <= stacked_pos[None, :, None]
    scores = jnp.where(visible, scores, -1e30)
    new_max = jnp.maximum(running_max, jnp.max(scores, axis=2))
    weights = jnp.where(visible, jnp.exp(scores - new_max[..., None]), 0.0)
    new_sum = jnp.sum(weights, axis=2)
    product = jnp.einsum(
        "grk,kgd->grd",
        weights.astype(jnp.bfloat16),
        value_heads,
        preferred_element_type=jnp.float32,
    )
    attended = (product / new_sum[..., None]).astype(jnp.bfloat16)
    attended = attended.reshape(local_groups, query_head_group, row_count, HEAD_SIZE).transpose(
        2, 0, 1, 3
    )
    attended = attended.reshape(row_count, local_groups * query_head_group * HEAD_SIZE)

    total = None
    for piece, sources in ((0, sources_a), (1, sources_b)):
        for which, held in ((0, mine_weights), (1, other_weights)):
            piece_t = held[piece * row_count : (piece + 1) * row_count]
            piece_t = jnp.swapaxes(piece_t, 0, 1).reshape(context_size, weight_cols, quarter)
            owner = core if which == 0 else 1 - core
            piece_rows = lax.dynamic_slice_in_dim(
                attended, owner * half_rows + piece * quarter, quarter, 1
            )
            product_out = jnp.einsum(
                "rh,nkh->rnk", piece_rows, piece_t, preferred_element_type=jnp.float32
            ).reshape(row_count, -1)
            product_out = context_order(
                product_out.reshape(row_count, context_size, -1), sources, x_size
            ).reshape(row_count, -1)
            total = product_out if total is None else total + product_out
    partial_out = total
    tensor_size = lax.axis_size("tensor")
    pieces = partial_out.astype(jnp.bfloat16).reshape(row_count, tensor_size, -1)
    pieces = lax.all_to_all(pieces, "tensor", 1, 1, tiled=True)
    return jnp.sum(pieces.astype(jnp.float32), axis=1).astype(jnp.bfloat16)


def solution(mesh):
    placed = (
        P(("dp", "context"), "tensor"),
        P(("dp", "context"), "tensor"),
        P(("dp", "context"), "tensor"),
        P("dp"),
        P("tensor", "context"),
    )
    return jax.shard_map(
        per_device,
        mesh=mesh,
        in_specs=placed,
        out_specs=P(("dp", "context"), "tensor"),
        check_vma=False,
    )
```

```python
import math

import jax
import jax.numpy as jnp
from jax import lax
from jax.sharding import PartitionSpec as P

QUERY_HEADS = 32
KEY_VALUE_HEADS = 8
HEAD_SIZE = 128
X_SIZE = 4


def chain_plan(context_size, x_size, x_first_mask):
    y_bits = [x_size << k for k in range((context_size // x_size).bit_length() - 1)][::-1]
    steps = [(bit, bit) for bit in y_bits]
    if x_size == 4:
        steps += [(1, 1), (3, 2)] if x_first_mask == 1 else [(3, 2), (1, 3)]
    else:
        steps += [(1 << k, 1 << k) for k in range(x_size.bit_length() - 1)]
    return steps


def upper_of(index, mask):
    bits = index & mask
    parity = jnp.zeros_like(index)
    for k in range(mask.bit_length()):
        parity = parity ^ ((bits >> k) & 1)
    return parity != 0


def upper_static(index, mask):
    return bin(index & mask).count("1") % 2 == 1


def stacked_sources(context_size, steps):
    lists = [[c] for c in range(context_size)]
    for mask, side in steps:
        lists = [
            (lists[c ^ mask] + lists[c]) if upper_static(c, side) else (lists[c] + lists[c ^ mask])
            for c in range(context_size)
        ]
    assert all(entry == lists[0] for entry in lists)
    return lists[0]


def exchange_gather(block, steps, axis_name, count, axis=1):
    index = lax.axis_index(axis_name)
    stack = block
    for mask, side in steps:
        received = lax.ppermute(stack, axis_name, [(i, i ^ mask) for i in range(count)])
        stack = jnp.where(
            upper_of(index, side),
            jnp.concatenate([received, stack], axis),
            jnp.concatenate([stack, received], axis),
        )
    return stack


def unpermute_blocks(product, sources, x_size):
    rows = product.shape[0]
    count = len(sources)
    y_count = count // x_size
    x_order = [sources[ix * y_count] % x_size for ix in range(x_size)]
    y_order = [sources[iy] // x_size for iy in range(y_count)]
    assert all(
        sources[ix * y_count + iy] == y_order[iy] * x_size + x_order[ix]
        for ix in range(x_size)
        for iy in range(y_count)
    )
    product = product.reshape(rows, x_size, y_count, -1)
    x_inverse = [x_order.index(x) for x in range(x_size)]
    y_inverse = [y_order.index(y) for y in range(y_count)]
    if x_inverse != list(range(x_size)):
        product = jnp.concatenate([product[:, i : i + 1] for i in x_inverse], axis=1)
    if y_inverse != list(range(y_count)):
        product = jnp.concatenate([product[:, :, i : i + 1] for i in y_inverse], axis=2)
    return jnp.swapaxes(product, 1, 2).reshape(rows, -1)


def exchange_gather_pair(stack_a, steps_a, stack_b, steps_b, axis_name, count):
    index = lax.axis_index(axis_name)
    for (mask_a, side_a), (mask_b, side_b) in zip(steps_a, steps_b):
        received_a = lax.ppermute(stack_a, axis_name, [(i, i ^ mask_a) for i in range(count)])
        received_b = lax.ppermute(stack_b, axis_name, [(i, i ^ mask_b) for i in range(count)])
        stack_a = jnp.where(
            upper_of(index, side_a),
            jnp.concatenate([received_a, stack_a], 1),
            jnp.concatenate([stack_a, received_a], 1),
        )
        stack_b = jnp.where(
            upper_of(index, side_b),
            jnp.concatenate([received_b, stack_b], 1),
            jnp.concatenate([stack_b, received_b], 1),
        )
        stack_a, stack_b = lax.optimization_barrier((stack_a, stack_b))
    return stack_a, stack_b


def restack(stack, sources, target, x_size):
    rows, count = stack.shape[:2]
    y_count = count // x_size
    x_from = [sources[ix * y_count] for ix in range(x_size)]
    x_to = [target[ix * y_count] for ix in range(x_size)]
    assert all(
        sources[ix * y_count + iy] - x_from[ix] == target[ix * y_count + iy] - x_to[ix]
        for ix in range(x_size)
        for iy in range(y_count)
    )
    picks = [x_from.index(x) for x in x_to]
    if picks == list(range(x_size)):
        return stack
    stack = stack.reshape(rows, x_size, y_count, -1)
    stack = jnp.concatenate([stack[:, i : i + 1] for i in picks], axis=1)
    return stack.reshape(rows, count, -1)


def per_device(queries, keys, values, order, out_weight):
    row_count = queries.shape[0]
    local_groups = keys.shape[1] // HEAD_SIZE
    query_head_group = QUERY_HEADS // KEY_VALUE_HEADS
    score_scale = 1.0 / math.sqrt(HEAD_SIZE)
    context_size = lax.axis_size("context")
    dp_size = lax.axis_size("dp")
    x_size = X_SIZE if context_size % X_SIZE == 0 and context_size > X_SIZE else 1

    core = lax.axis_index("dp") % 2
    weight_rows, weight_cols = out_weight.shape
    half_rows = weight_rows // 2
    quarter = half_rows // 2
    mine = lax.dynamic_slice_in_dim(out_weight, core * half_rows, half_rows, 0)
    steps_a = chain_plan(context_size, x_size, 1)
    steps_b = chain_plan(context_size, x_size, 3)
    shared = 0
    while shared < min(len(steps_a), len(steps_b)) and steps_a[shared] == steps_b[shared]:
        shared += 1
    key_width = keys.shape[1]
    quarters = [
        mine[k * quarter : (k + 1) * quarter].T.reshape(row_count, -1) for k in range(2)
    ]
    block = jnp.stack(
        [
            jnp.concatenate([keys, quarters[0]], axis=1)[:, None, :],
            jnp.concatenate([values, quarters[1]], axis=1)[:, None, :],
        ]
    )
    gathered = exchange_gather(block, steps_a[:shared], "context", context_size, axis=2)
    gathered_a, gathered_b = exchange_gather_pair(
        gathered[0],
        steps_a[shared:],
        gathered[1],
        steps_b[shared:],
        "context",
        context_size,
    )
    sources_a = stacked_sources(context_size, steps_a)
    sources_b = stacked_sources(context_size, steps_b)

    mine_weights = jnp.concatenate(
        [gathered_a[:, :, key_width:], gathered_b[:, :, values.shape[1] :]], axis=0
    )
    other_weights = lax.ppermute(mine_weights, "dp", [(i, i ^ 1) for i in range(dp_size)])

    key_stack = gathered_a[:, :, :key_width]
    value_stack = restack(gathered_b[:, :, : values.shape[1]], sources_b, sources_a, x_size)
    key_part = jnp.swapaxes(key_stack, 0, 1).reshape(context_size * row_count, key_width)
    value_part = jnp.swapaxes(value_stack, 0, 1).reshape(context_size * row_count, -1)
    key_pos = order.reshape(context_size, row_count)[jnp.array(sources_a)].reshape(-1)

    first_row = lax.axis_index("context") * row_count
    query_pos = lax.dynamic_slice_in_dim(order, first_row, row_count, 0)
    stacked = queries.reshape(row_count, local_groups, query_head_group, HEAD_SIZE)
    stacked = stacked.transpose(1, 2, 0, 3).reshape(
        local_groups, query_head_group * row_count, HEAD_SIZE
    )
    stacked_pos = jnp.tile(query_pos, query_head_group)
    stacked_rows = query_head_group * row_count
    key_count = key_part.shape[0]
    running_max = jnp.full((local_groups, stacked_rows), -1e30, jnp.float32)
    key_heads = key_part.reshape(key_count, local_groups, HEAD_SIZE)
    value_heads = value_part.reshape(key_count, local_groups, HEAD_SIZE)
    scores = (
        jnp.einsum("grd,kgd->grk", stacked, key_heads, preferred_element_type=jnp.float32)
        * score_scale
    )
    visible = key_pos[None, None, :] <= stacked_pos[None, :, None]
    scores = jnp.where(visible, scores, -1e30)
    new_max = jnp.maximum(running_max, jnp.max(scores, axis=2))
    weights = jnp.where(visible, jnp.exp(scores - new_max[..., None]), 0.0)
    new_sum = jnp.sum(weights, axis=2)
    product = jnp.einsum(
        "grk,kgd->grd",
        weights.astype(jnp.bfloat16),
        value_heads,
        preferred_element_type=jnp.float32,
    )
    attended = (product / new_sum[..., None]).astype(jnp.bfloat16)
    attended = attended.reshape(local_groups, query_head_group, row_count, HEAD_SIZE).transpose(
        2, 0, 1, 3
    )
    attended = attended.reshape(row_count, local_groups * query_head_group * HEAD_SIZE)

    total = None
    for piece, sources in ((0, sources_a), (1, sources_b)):
        for which, held in ((0, mine_weights), (1, other_weights)):
            piece_t = held[piece * row_count : (piece + 1) * row_count]
            piece_t = jnp.swapaxes(piece_t, 0, 1).reshape(context_size, weight_cols, quarter)
            owner = core if which == 0 else 1 - core
            piece_rows = lax.dynamic_slice_in_dim(
                attended, owner * half_rows + piece * quarter, quarter, 1
            )
            product_out = jnp.einsum(
                "rh,nkh->rnk", piece_rows, piece_t, preferred_element_type=jnp.float32
            ).reshape(row_count, -1)
            product_out = unpermute_blocks(product_out, sources, x_size)
            total = product_out if total is None else total + product_out
    partial_out = total
    tensor_size = lax.axis_size("tensor")
    pieces = partial_out.astype(jnp.bfloat16).reshape(row_count, tensor_size, -1)
    pieces = lax.all_to_all(pieces, "tensor", 1, 1, tiled=True)
    return jnp.sum(pieces.astype(jnp.float32), axis=1).astype(jnp.bfloat16)


def solution(mesh):
    placed = (
        P(("dp", "context"), "tensor"),
        P(("dp", "context"), "tensor"),
        P(("dp", "context"), "tensor"),
        P("dp"),
        P("tensor", "context"),
    )
    return jax.shard_map(
        per_device,
        mesh=mesh,
        in_specs=placed,
        out_specs=P(("dp", "context"), "tensor"),
        check_vma=False,
    )
```

```python
import math

import jax
import jax.numpy as jnp
from jax import lax
from jax.sharding import PartitionSpec as P

QUERY_HEADS = 32
KEY_VALUE_HEADS = 8
HEAD_SIZE = 128
X_SIZE = 4


def chain_plan(context_size, x_size, x_first_mask):
    y_bits = [x_size << k for k in range((context_size // x_size).bit_length() - 1)][::-1]
    steps = [(bit, bit) for bit in y_bits]
    if x_size == 4:
        steps += [(1, 1), (3, 2)] if x_first_mask == 1 else [(3, 2), (1, 3)]
    else:
        steps += [(1 << k, 1 << k) for k in range(x_size.bit_length() - 1)]
    return steps


def upper_of(index, mask):
    bits = index & mask
    parity = jnp.zeros_like(index)
    for k in range(mask.bit_length()):
        parity = parity ^ ((bits >> k) & 1)
    return parity != 0


def upper_static(index, mask):
    return bin(index & mask).count("1") % 2 == 1


def stacked_sources(context_size, steps):
    lists = [[c] for c in range(context_size)]
    for mask, side in steps:
        lists = [
            (lists[c ^ mask] + lists[c]) if upper_static(c, side) else (lists[c] + lists[c ^ mask])
            for c in range(context_size)
        ]
    assert all(entry == lists[0] for entry in lists)
    return lists[0]


def exchange_gather(block, steps, axis_name, count):
    index = lax.axis_index(axis_name)
    stack = block
    for mask, side in steps:
        received = lax.ppermute(stack, axis_name, [(i, i ^ mask) for i in range(count)])
        stack = jnp.where(
            upper_of(index, side),
            jnp.concatenate([received, stack], 1),
            jnp.concatenate([stack, received], 1),
        )
    return stack


def unpermute_blocks(product, sources, x_size):
    rows = product.shape[0]
    count = len(sources)
    y_count = count // x_size
    x_order = [sources[ix * y_count] % x_size for ix in range(x_size)]
    y_order = [sources[iy] // x_size for iy in range(y_count)]
    assert all(
        sources[ix * y_count + iy] == y_order[iy] * x_size + x_order[ix]
        for ix in range(x_size)
        for iy in range(y_count)
    )
    product = product.reshape(rows, x_size, y_count, -1)
    x_inverse = [x_order.index(x) for x in range(x_size)]
    y_inverse = [y_order.index(y) for y in range(y_count)]
    if x_inverse != list(range(x_size)):
        product = jnp.concatenate([product[:, i : i + 1] for i in x_inverse], axis=1)
    if y_inverse != list(range(y_count)):
        product = jnp.concatenate([product[:, :, i : i + 1] for i in y_inverse], axis=2)
    return jnp.swapaxes(product, 1, 2).reshape(rows, -1)


def exchange_gather_pair(stack_a, steps_a, stack_b, steps_b, axis_name, count):
    index = lax.axis_index(axis_name)
    for (mask_a, side_a), (mask_b, side_b) in zip(steps_a, steps_b):
        received_a = lax.ppermute(stack_a, axis_name, [(i, i ^ mask_a) for i in range(count)])
        received_b = lax.ppermute(stack_b, axis_name, [(i, i ^ mask_b) for i in range(count)])
        stack_a = jnp.where(
            upper_of(index, side_a),
            jnp.concatenate([received_a, stack_a], 1),
            jnp.concatenate([stack_a, received_a], 1),
        )
        stack_b = jnp.where(
            upper_of(index, side_b),
            jnp.concatenate([received_b, stack_b], 1),
            jnp.concatenate([stack_b, received_b], 1),
        )
        stack_a, stack_b = lax.optimization_barrier((stack_a, stack_b))
    return stack_a, stack_b


def exchange_last_pair(stack_a, step_a, stack_b, step_b, axis_name, count):
    index = lax.axis_index(axis_name)
    (mask_a, side_a), (mask_b, side_b) = step_a, step_b
    received_a = lax.ppermute(stack_a, axis_name, [(i, i ^ mask_a) for i in range(count)])
    received_b = lax.ppermute(stack_b, axis_name, [(i, i ^ mask_b) for i in range(count)])
    return (
        jnp.concatenate([stack_a, received_a], 1),
        jnp.concatenate([stack_b, received_b], 1),
        upper_of(index, side_a),
        upper_of(index, side_b),
    )


def swap_halves(stack, upper):
    half = stack.shape[1] // 2
    return jnp.where(upper, jnp.concatenate([stack[:, half:], stack[:, :half]], 1), stack)


def restack(stack, sources, target, x_size):
    rows, count = stack.shape[:2]
    y_count = count // x_size
    x_from = [sources[ix * y_count] for ix in range(x_size)]
    x_to = [target[ix * y_count] for ix in range(x_size)]
    assert all(
        sources[ix * y_count + iy] - x_from[ix] == target[ix * y_count + iy] - x_to[ix]
        for ix in range(x_size)
        for iy in range(y_count)
    )
    picks = [x_from.index(x) for x in x_to]
    if picks == list(range(x_size)):
        return stack
    stack = stack.reshape(rows, x_size, y_count, -1)
    stack = jnp.concatenate([stack[:, i : i + 1] for i in picks], axis=1)
    return stack.reshape(rows, count, -1)


def per_device(queries, keys, values, order, out_weight):
    row_count = queries.shape[0]
    local_groups = keys.shape[1] // HEAD_SIZE
    query_head_group = QUERY_HEADS // KEY_VALUE_HEADS
    score_scale = 1.0 / math.sqrt(HEAD_SIZE)
    context_size = lax.axis_size("context")
    dp_size = lax.axis_size("dp")
    x_size = X_SIZE if context_size % X_SIZE == 0 and context_size > X_SIZE else 1

    core = lax.axis_index("dp") % 2
    weight_rows, weight_cols = out_weight.shape
    half_rows = weight_rows // 2
    quarter = half_rows // 2
    mine = lax.dynamic_slice_in_dim(out_weight, core * half_rows, half_rows, 0)
    steps_a = chain_plan(context_size, x_size, 1)
    steps_b = chain_plan(context_size, x_size, 3)
    shared = 0
    while shared < min(len(steps_a), len(steps_b)) and steps_a[shared] == steps_b[shared]:
        shared += 1
    key_width = keys.shape[1]
    quarters = [
        mine[k * quarter : (k + 1) * quarter].T.reshape(row_count, -1) for k in range(2)
    ]
    block = jnp.concatenate([keys, quarters[0], values, quarters[1]], axis=1)[:, None, :]
    gathered = exchange_gather(block, steps_a[:shared], "context", context_size)
    gathered_a, gathered_b = exchange_gather_pair(
        gathered[:, :, : key_width + weight_cols],
        steps_a[shared:-1],
        gathered[:, :, key_width + weight_cols :],
        steps_b[shared:-1],
        "context",
        context_size,
    )
    gathered_a, gathered_b, upper_a, upper_b = exchange_last_pair(
        gathered_a, steps_a[-1], gathered_b, steps_b[-1], "context", context_size
    )
    sources_a = stacked_sources(context_size, steps_a)
    sources_b = stacked_sources(context_size, steps_b)

    mine_weights = jnp.concatenate(
        [gathered_a[:, :, key_width:], gathered_b[:, :, values.shape[1] :]], axis=0
    )
    other_weights = lax.ppermute(mine_weights, "dp", [(i, i ^ 1) for i in range(dp_size)])

    key_stack = swap_halves(gathered_a[:, :, :key_width], upper_a)
    value_stack = swap_halves(gathered_b[:, :, : values.shape[1]], upper_b)
    value_stack = restack(value_stack, sources_b, sources_a, x_size)
    key_part = jnp.swapaxes(key_stack, 0, 1).reshape(context_size * row_count, key_width)
    value_part = jnp.swapaxes(value_stack, 0, 1).reshape(context_size * row_count, -1)
    key_pos = order.reshape(context_size, row_count)[jnp.array(sources_a)].reshape(-1)

    first_row = lax.axis_index("context") * row_count
    query_pos = lax.dynamic_slice_in_dim(order, first_row, row_count, 0)
    stacked = queries.reshape(row_count, local_groups, query_head_group, HEAD_SIZE)
    stacked = stacked.transpose(1, 2, 0, 3).reshape(
        local_groups, query_head_group * row_count, HEAD_SIZE
    )
    stacked_pos = jnp.tile(query_pos, query_head_group)
    stacked_rows = query_head_group * row_count
    key_count = key_part.shape[0]
    running_max = jnp.full((local_groups, stacked_rows), -1e30, jnp.float32)
    key_heads = key_part.reshape(key_count, local_groups, HEAD_SIZE)
    value_heads = value_part.reshape(key_count, local_groups, HEAD_SIZE)
    scores = (
        jnp.einsum("grd,kgd->grk", stacked, key_heads, preferred_element_type=jnp.float32)
        * score_scale
    )
    visible = key_pos[None, None, :] <= stacked_pos[None, :, None]
    scores = jnp.where(visible, scores, -1e30)
    new_max = jnp.maximum(running_max, jnp.max(scores, axis=2))
    weights = jnp.where(visible, jnp.exp(scores - new_max[..., None]), 0.0)
    new_sum = jnp.sum(weights, axis=2)
    product = jnp.einsum(
        "grk,kgd->grd",
        weights.astype(jnp.bfloat16),
        value_heads,
        preferred_element_type=jnp.float32,
    )
    attended = (product / new_sum[..., None]).astype(jnp.bfloat16)
    attended = attended.reshape(local_groups, query_head_group, row_count, HEAD_SIZE).transpose(
        2, 0, 1, 3
    )
    attended = attended.reshape(row_count, local_groups * query_head_group * HEAD_SIZE)

    total = None
    for piece, sources, upper in ((0, sources_a, upper_a), (1, sources_b, upper_b)):
        half = context_size // 2
        swapped = sources[half:] + sources[:half]
        for which, held in ((0, mine_weights), (1, other_weights)):
            piece_t = held[piece * row_count : (piece + 1) * row_count]
            piece_t = jnp.swapaxes(piece_t, 0, 1).reshape(context_size, weight_cols, quarter)
            owner = core if which == 0 else 1 - core
            piece_rows = lax.dynamic_slice_in_dim(
                attended, owner * half_rows + piece * quarter, quarter, 1
            )
            product_out = jnp.einsum(
                "rh,nkh->rnk", piece_rows, piece_t, preferred_element_type=jnp.float32
            ).reshape(row_count, -1)
            product_out = jnp.where(
                upper,
                unpermute_blocks(product_out, swapped, x_size),
                unpermute_blocks(product_out, sources, x_size),
            )
            total = product_out if total is None else total + product_out
    partial_out = total
    tensor_size = lax.axis_size("tensor")
    pieces = partial_out.astype(jnp.bfloat16).reshape(row_count, tensor_size, -1)
    pieces = lax.all_to_all(pieces, "tensor", 1, 1, tiled=True)
    return jnp.sum(pieces.astype(jnp.float32), axis=1).astype(jnp.bfloat16)


def solution(mesh):
    placed = (
        P(("dp", "context"), "tensor"),
        P(("dp", "context"), "tensor"),
        P(("dp", "context"), "tensor"),
        P("dp"),
        P("tensor", "context"),
    )
    return jax.shard_map(
        per_device,
        mesh=mesh,
        in_specs=placed,
        out_specs=P(("dp", "context"), "tensor"),
        check_vma=False,
    )
```

```python
import math

import jax
import jax.numpy as jnp
from jax import lax
from jax.sharding import PartitionSpec as P

QUERY_HEADS = 32
KEY_VALUE_HEADS = 8
HEAD_SIZE = 128
X_SIZE = 4


def chain_plan(context_size, x_size, x_first_mask):
    y_bits = [x_size << k for k in range((context_size // x_size).bit_length() - 1)][::-1]
    steps = [(bit, bit) for bit in y_bits]
    if x_size == 4:
        steps += [(1, 1), (3, 2)] if x_first_mask == 1 else [(3, 2), (1, 3)]
    else:
        steps += [(1 << k, 1 << k) for k in range(x_size.bit_length() - 1)]
    return steps


def upper_of(index, mask):
    bits = index & mask
    parity = jnp.zeros_like(index)
    for k in range(mask.bit_length()):
        parity = parity ^ ((bits >> k) & 1)
    return parity != 0


def upper_static(index, mask):
    return bin(index & mask).count("1") % 2 == 1


def stacked_sources(context_size, steps):
    lists = [[c] for c in range(context_size)]
    for mask, side in steps:
        lists = [
            (lists[c ^ mask] + lists[c]) if upper_static(c, side) else (lists[c] + lists[c ^ mask])
            for c in range(context_size)
        ]
    assert all(entry == lists[0] for entry in lists)
    return lists[0]


def exchange_gather(block, steps, axis_name, count):
    index = lax.axis_index(axis_name)
    stack = block
    for mask, side in steps:
        received = lax.ppermute(stack, axis_name, [(i, i ^ mask) for i in range(count)])
        stack = jnp.where(
            upper_of(index, side),
            jnp.concatenate([received, stack], 1),
            jnp.concatenate([stack, received], 1),
        )
    return stack


def unpermute_blocks(product, sources, x_size):
    rows = product.shape[0]
    count = len(sources)
    y_count = count // x_size
    x_order = [sources[ix * y_count] % x_size for ix in range(x_size)]
    y_order = [sources[iy] // x_size for iy in range(y_count)]
    assert all(
        sources[ix * y_count + iy] == y_order[iy] * x_size + x_order[ix]
        for ix in range(x_size)
        for iy in range(y_count)
    )
    product = product.reshape(rows, x_size, y_count, -1)
    x_inverse = [x_order.index(x) for x in range(x_size)]
    y_inverse = [y_order.index(y) for y in range(y_count)]
    if x_inverse != list(range(x_size)):
        product = jnp.concatenate([product[:, i : i + 1] for i in x_inverse], axis=1)
    if y_inverse != list(range(y_count)):
        product = jnp.concatenate([product[:, :, i : i + 1] for i in y_inverse], axis=2)
    return jnp.swapaxes(product, 1, 2).reshape(rows, -1)


def exchange_gather_pair(stack_a, steps_a, stack_b, steps_b, axis_name, count):
    index = lax.axis_index(axis_name)
    for step, ((mask_a, side_a), (mask_b, side_b)) in enumerate(zip(steps_a, steps_b)):
        received_a = lax.ppermute(stack_a, axis_name, [(i, i ^ mask_a) for i in range(count)])
        received_b = lax.ppermute(stack_b, axis_name, [(i, i ^ mask_b) for i in range(count)])
        stack_a = jnp.where(
            upper_of(index, side_a),
            jnp.concatenate([received_a, stack_a], 1),
            jnp.concatenate([stack_a, received_a], 1),
        )
        stack_b = jnp.where(
            upper_of(index, side_b),
            jnp.concatenate([received_b, stack_b], 1),
            jnp.concatenate([stack_b, received_b], 1),
        )
        if step + 1 < len(steps_a):
            stack_a, stack_b = lax.optimization_barrier((stack_a, stack_b))
    return stack_a, stack_b


def restack(stack, sources, target, x_size):
    rows, count = stack.shape[:2]
    y_count = count // x_size
    x_from = [sources[ix * y_count] for ix in range(x_size)]
    x_to = [target[ix * y_count] for ix in range(x_size)]
    assert all(
        sources[ix * y_count + iy] - x_from[ix] == target[ix * y_count + iy] - x_to[ix]
        for ix in range(x_size)
        for iy in range(y_count)
    )
    picks = [x_from.index(x) for x in x_to]
    if picks == list(range(x_size)):
        return stack
    stack = stack.reshape(rows, x_size, y_count, -1)
    stack = jnp.concatenate([stack[:, i : i + 1] for i in picks], axis=1)
    return stack.reshape(rows, count, -1)


def per_device(queries, keys, values, order, out_weight):
    row_count = queries.shape[0]
    local_groups = keys.shape[1] // HEAD_SIZE
    query_head_group = QUERY_HEADS // KEY_VALUE_HEADS
    score_scale = 1.0 / math.sqrt(HEAD_SIZE)
    context_size = lax.axis_size("context")
    dp_size = lax.axis_size("dp")
    x_size = X_SIZE if context_size % X_SIZE == 0 and context_size > X_SIZE else 1

    core = lax.axis_index("dp") % 2
    weight_rows, weight_cols = out_weight.shape
    half_rows = weight_rows // 2
    quarter = half_rows // 2
    mine = lax.dynamic_slice_in_dim(out_weight, core * half_rows, half_rows, 0)
    steps_a = chain_plan(context_size, x_size, 1)
    steps_b = chain_plan(context_size, x_size, 3)
    shared = 0
    while shared < min(len(steps_a), len(steps_b)) and steps_a[shared] == steps_b[shared]:
        shared += 1
    key_width = keys.shape[1]
    quarters = [
        mine[k * quarter : (k + 1) * quarter].T.reshape(row_count, -1) for k in range(2)
    ]
    block = jnp.concatenate([keys, quarters[0], values, quarters[1]], axis=1)[:, None, :]
    gathered = exchange_gather(block, steps_a[:shared], "context", context_size)
    gathered_a, gathered_b = exchange_gather_pair(
        gathered[:, :, : key_width + weight_cols],
        steps_a[shared:],
        gathered[:, :, key_width + weight_cols :],
        steps_b[shared:],
        "context",
        context_size,
    )
    sources_a = stacked_sources(context_size, steps_a)
    sources_b = stacked_sources(context_size, steps_b)

    mine_weights = jnp.concatenate(
        [gathered_a[:, :, key_width:], gathered_b[:, :, values.shape[1] :]], axis=0
    )
    other_weights = lax.ppermute(mine_weights, "dp", [(i, i ^ 1) for i in range(dp_size)])

    key_stack = gathered_a[:, :, :key_width]
    value_stack = restack(gathered_b[:, :, : values.shape[1]], sources_b, sources_a, x_size)
    key_part = jnp.swapaxes(key_stack, 0, 1).reshape(context_size * row_count, key_width)
    value_part = jnp.swapaxes(value_stack, 0, 1).reshape(context_size * row_count, -1)
    key_pos = order.reshape(context_size, row_count)[jnp.array(sources_a)].reshape(-1)

    first_row = lax.axis_index("context") * row_count
    query_pos = lax.dynamic_slice_in_dim(order, first_row, row_count, 0)
    stacked = queries.reshape(row_count, local_groups, query_head_group, HEAD_SIZE)
    stacked = stacked.transpose(1, 2, 0, 3).reshape(
        local_groups, query_head_group * row_count, HEAD_SIZE
    )
    stacked_pos = jnp.tile(query_pos, query_head_group)
    stacked_rows = query_head_group * row_count
    key_count = key_part.shape[0]
    running_max = jnp.full((local_groups, stacked_rows), -1e30, jnp.float32)
    key_heads = key_part.reshape(key_count, local_groups, HEAD_SIZE)
    value_heads = value_part.reshape(key_count, local_groups, HEAD_SIZE)
    scores = (
        jnp.einsum("grd,kgd->grk", stacked, key_heads, preferred_element_type=jnp.float32)
        * score_scale
    )
    visible = key_pos[None, None, :] <= stacked_pos[None, :, None]
    scores = jnp.where(visible, scores, -1e30)
    new_max = jnp.maximum(running_max, jnp.max(scores, axis=2))
    weights = jnp.where(visible, jnp.exp(scores - new_max[..., None]), 0.0)
    new_sum = jnp.sum(weights, axis=2)
    product = jnp.einsum(
        "grk,kgd->grd",
        weights.astype(jnp.bfloat16),
        value_heads,
        preferred_element_type=jnp.float32,
    )
    attended = (product / new_sum[..., None]).astype(jnp.bfloat16)
    attended = attended.reshape(local_groups, query_head_group, row_count, HEAD_SIZE).transpose(
        2, 0, 1, 3
    )
    attended = attended.reshape(row_count, local_groups * query_head_group * HEAD_SIZE)

    total = None
    for piece, sources in ((0, sources_a), (1, sources_b)):
        for which, held in ((0, mine_weights), (1, other_weights)):
            piece_t = held[piece * row_count : (piece + 1) * row_count]
            piece_t = jnp.swapaxes(piece_t, 0, 1).reshape(context_size, weight_cols, quarter)
            owner = core if which == 0 else 1 - core
            piece_rows = lax.dynamic_slice_in_dim(
                attended, owner * half_rows + piece * quarter, quarter, 1
            )
            product_out = jnp.einsum(
                "rh,nkh->rnk", piece_rows, piece_t, preferred_element_type=jnp.float32
            ).reshape(row_count, -1)
            product_out = unpermute_blocks(product_out, sources, x_size)
            total = product_out if total is None else total + product_out
    partial_out = total
    tensor_size = lax.axis_size("tensor")
    pieces = partial_out.astype(jnp.bfloat16).reshape(row_count, tensor_size, -1)
    pieces = lax.all_to_all(pieces, "tensor", 1, 1, tiled=True)
    return jnp.sum(pieces.astype(jnp.float32), axis=1).astype(jnp.bfloat16)


def solution(mesh):
    placed = (
        P(("dp", "context"), "tensor"),
        P(("dp", "context"), "tensor"),
        P(("dp", "context"), "tensor"),
        P("dp"),
        P("tensor", "context"),
    )
    return jax.shard_map(
        per_device,
        mesh=mesh,
        in_specs=placed,
        out_specs=P(("dp", "context"), "tensor"),
        check_vma=False,
    )
```

```python
import math

import jax
import jax.numpy as jnp
from jax import lax
from jax.sharding import PartitionSpec as P

QUERY_HEADS = 32
KEY_VALUE_HEADS = 8
HEAD_SIZE = 128
X_SIZE = 4


def chain_plan(context_size, x_size, x_first_mask):
    y_bits = [x_size << k for k in range((context_size // x_size).bit_length() - 1)][::-1]
    steps = [(bit, bit) for bit in y_bits]
    if x_size == 4:
        steps += [(1, 1), (3, 2)] if x_first_mask == 1 else [(3, 2), (1, 3)]
    else:
        steps += [(1 << k, 1 << k) for k in range(x_size.bit_length() - 1)]
    return steps


def upper_of(index, mask):
    bits = index & mask
    parity = jnp.zeros_like(index)
    for k in range(mask.bit_length()):
        parity = parity ^ ((bits >> k) & 1)
    return parity != 0


def upper_static(index, mask):
    return bin(index & mask).count("1") % 2 == 1


def stacked_sources(context_size, steps):
    lists = [[c] for c in range(context_size)]
    for mask, side in steps:
        lists = [
            (lists[c ^ mask] + lists[c]) if upper_static(c, side) else (lists[c] + lists[c ^ mask])
            for c in range(context_size)
        ]
    assert all(entry == lists[0] for entry in lists)
    return lists[0]


def exchange_gather(block, steps, axis_name, count):
    index = lax.axis_index(axis_name)
    stack = block
    for mask, side in steps:
        received = lax.ppermute(stack, axis_name, [(i, i ^ mask) for i in range(count)])
        stack = jnp.where(
            upper_of(index, side),
            jnp.concatenate([received, stack], 1),
            jnp.concatenate([stack, received], 1),
        )
    return stack


def unpermute_blocks(product, sources, x_size):
    rows = product.shape[0]
    count = len(sources)
    y_count = count // x_size
    x_order = [sources[ix * y_count] % x_size for ix in range(x_size)]
    y_order = [sources[iy] // x_size for iy in range(y_count)]
    assert all(
        sources[ix * y_count + iy] == y_order[iy] * x_size + x_order[ix]
        for ix in range(x_size)
        for iy in range(y_count)
    )
    product = product.reshape(rows, x_size, y_count, -1)
    x_inverse = [x_order.index(x) for x in range(x_size)]
    y_inverse = [y_order.index(y) for y in range(y_count)]
    if x_inverse != list(range(x_size)):
        product = jnp.concatenate([product[:, i : i + 1] for i in x_inverse], axis=1)
    if y_inverse != list(range(y_count)):
        product = jnp.concatenate([product[:, :, i : i + 1] for i in y_inverse], axis=2)
    return jnp.swapaxes(product, 1, 2).reshape(rows, -1)


def exchange_gather_pair(stack_a, steps_a, stack_b, steps_b, axis_name, count):
    index = lax.axis_index(axis_name)
    for (mask_a, side_a), (mask_b, side_b) in zip(steps_a, steps_b):
        received_a = lax.ppermute(stack_a, axis_name, [(i, i ^ mask_a) for i in range(count)])
        received_b = lax.ppermute(stack_b, axis_name, [(i, i ^ mask_b) for i in range(count)])
        stack_a = jnp.where(
            upper_of(index, side_a),
            jnp.concatenate([received_a, stack_a], 1),
            jnp.concatenate([stack_a, received_a], 1),
        )
        stack_b = jnp.where(
            upper_of(index, side_b),
            jnp.concatenate([received_b, stack_b], 1),
            jnp.concatenate([stack_b, received_b], 1),
        )
        stack_a, stack_b = lax.optimization_barrier((stack_a, stack_b))
    return stack_a, stack_b


def restack(stack, sources, target, x_size):
    rows, count = stack.shape[:2]
    y_count = count // x_size
    x_from = [sources[ix * y_count] for ix in range(x_size)]
    x_to = [target[ix * y_count] for ix in range(x_size)]
    assert all(
        sources[ix * y_count + iy] - x_from[ix] == target[ix * y_count + iy] - x_to[ix]
        for ix in range(x_size)
        for iy in range(y_count)
    )
    picks = [x_from.index(x) for x in x_to]
    if picks == list(range(x_size)):
        return stack
    stack = stack.reshape(rows, x_size, y_count, -1)
    stack = jnp.concatenate([stack[:, i : i + 1] for i in picks], axis=1)
    return stack.reshape(rows, count, -1)


def per_device(queries, keys, values, order, out_weight):
    row_count = queries.shape[0]
    local_groups = keys.shape[1] // HEAD_SIZE
    query_head_group = QUERY_HEADS // KEY_VALUE_HEADS
    score_scale = 1.0 / math.sqrt(HEAD_SIZE)
    context_size = lax.axis_size("context")
    dp_size = lax.axis_size("dp")
    x_size = X_SIZE if context_size % X_SIZE == 0 and context_size > X_SIZE else 1

    core = lax.axis_index("dp") % 2
    weight_rows, weight_cols = out_weight.shape
    half_rows = weight_rows // 2
    quarter = half_rows // 2
    mine = lax.dynamic_slice_in_dim(out_weight, core * half_rows, half_rows, 0)
    steps_a = chain_plan(context_size, x_size, 1)
    steps_b = chain_plan(context_size, x_size, 3)
    shared = 0
    while shared < min(len(steps_a), len(steps_b)) and steps_a[shared] == steps_b[shared]:
        shared += 1
    key_width = keys.shape[1]
    quarters = [
        mine[k * quarter : (k + 1) * quarter].T.reshape(row_count, -1) for k in range(2)
    ]
    block = jnp.concatenate([keys, quarters[0], values, quarters[1]], axis=1)[:, None, :]
    gathered = exchange_gather(block, steps_a[:shared], "context", context_size)
    gathered_a, gathered_b = exchange_gather_pair(
        gathered[:, :, : key_width + weight_cols],
        steps_a[shared:],
        gathered[:, :, key_width + weight_cols :],
        steps_b[shared:],
        "context",
        context_size,
    )
    sources_a = stacked_sources(context_size, steps_a)
    sources_b = stacked_sources(context_size, steps_b)

    mine_weights = jnp.concatenate(
        [gathered_a[:, :, key_width:], gathered_b[:, :, values.shape[1] :]], axis=0
    )
    other_weights = lax.ppermute(mine_weights, "dp", [(i, i ^ 1) for i in range(dp_size)])

    whole_rows = local_groups == 1
    key_stack = gathered_a if whole_rows else gathered_a[:, :, :key_width]
    value_stack = restack(gathered_b[:, :, : values.shape[1]], sources_b, sources_a, x_size)
    key_part = jnp.swapaxes(key_stack, 0, 1).reshape(context_size * row_count, -1)
    value_part = jnp.swapaxes(value_stack, 0, 1).reshape(context_size * row_count, -1)
    key_pos = order.reshape(context_size, row_count)[jnp.array(sources_a)].reshape(-1)

    first_row = lax.axis_index("context") * row_count
    query_pos = lax.dynamic_slice_in_dim(order, first_row, row_count, 0)
    stacked = queries.reshape(row_count, local_groups, query_head_group, HEAD_SIZE)
    stacked = stacked.transpose(1, 2, 0, 3).reshape(
        local_groups, query_head_group * row_count, HEAD_SIZE
    )
    stacked_pos = jnp.tile(query_pos, query_head_group)
    stacked_rows = query_head_group * row_count
    key_count = key_part.shape[0]
    running_max = jnp.full((local_groups, stacked_rows), -1e30, jnp.float32)
    key_heads = key_part.reshape(key_count, local_groups, -1)
    if whole_rows:
        stacked = jnp.pad(stacked, ((0, 0), (0, 0), (0, key_heads.shape[2] - HEAD_SIZE)))
    value_heads = value_part.reshape(key_count, local_groups, HEAD_SIZE)
    scores = (
        jnp.einsum("grd,kgd->grk", stacked, key_heads, preferred_element_type=jnp.float32)
        * score_scale
    )
    visible = key_pos[None, None, :] <= stacked_pos[None, :, None]
    scores = jnp.where(visible, scores, -1e30)
    new_max = jnp.maximum(running_max, jnp.max(scores, axis=2))
    weights = jnp.where(visible, jnp.exp(scores - new_max[..., None]), 0.0)
    new_sum = jnp.sum(weights, axis=2)
    product = jnp.einsum(
        "grk,kgd->grd",
        weights.astype(jnp.bfloat16),
        value_heads,
        preferred_element_type=jnp.float32,
    )
    attended = (product / new_sum[..., None]).astype(jnp.bfloat16)
    attended = attended.reshape(local_groups, query_head_group, row_count, HEAD_SIZE).transpose(
        2, 0, 1, 3
    )
    attended = attended.reshape(row_count, local_groups * query_head_group * HEAD_SIZE)

    total = None
    for piece, sources in ((0, sources_a), (1, sources_b)):
        for which, held in ((0, mine_weights), (1, other_weights)):
            piece_t = held[piece * row_count : (piece + 1) * row_count]
            piece_t = jnp.swapaxes(piece_t, 0, 1).reshape(context_size, weight_cols, quarter)
            owner = core if which == 0 else 1 - core
            piece_rows = lax.dynamic_slice_in_dim(
                attended, owner * half_rows + piece * quarter, quarter, 1
            )
            product_out = jnp.einsum(
                "rh,nkh->rnk", piece_rows, piece_t, preferred_element_type=jnp.float32
            ).reshape(row_count, -1)
            product_out = unpermute_blocks(product_out, sources, x_size)
            total = product_out if total is None else total + product_out
    partial_out = total
    tensor_size = lax.axis_size("tensor")
    pieces = partial_out.astype(jnp.bfloat16).reshape(row_count, tensor_size, -1)
    pieces = lax.all_to_all(pieces, "tensor", 1, 1, tiled=True)
    return jnp.sum(pieces.astype(jnp.float32), axis=1).astype(jnp.bfloat16)


def solution(mesh):
    placed = (
        P(("dp", "context"), "tensor"),
        P(("dp", "context"), "tensor"),
        P(("dp", "context"), "tensor"),
        P("dp"),
        P("tensor", "context"),
    )
    return jax.shard_map(
        per_device,
        mesh=mesh,
        in_specs=placed,
        out_specs=P(("dp", "context"), "tensor"),
        check_vma=False,
    )
```

```python
import math

import jax
import jax.numpy as jnp
from jax import lax
from jax.sharding import PartitionSpec as P

QUERY_HEADS = 32
KEY_VALUE_HEADS = 8
HEAD_SIZE = 128
X_SIZE = 4


def chain_plan(context_size, x_size, x_first_mask):
    y_bits = [x_size << k for k in range((context_size // x_size).bit_length() - 1)][::-1]
    steps = [(bit, bit) for bit in y_bits]
    if x_size == 4:
        steps += [(1, 1), (3, 2)] if x_first_mask == 1 else [(3, 2), (1, 3)]
    else:
        steps += [(1 << k, 1 << k) for k in range(x_size.bit_length() - 1)]
    return steps


def upper_of(index, mask):
    bits = index & mask
    parity = jnp.zeros_like(index)
    for k in range(mask.bit_length()):
        parity = parity ^ ((bits >> k) & 1)
    return parity != 0


def upper_static(index, mask):
    return bin(index & mask).count("1") % 2 == 1


def stacked_sources(context_size, steps):
    lists = [[c] for c in range(context_size)]
    for mask, side in steps:
        lists = [
            (lists[c ^ mask] + lists[c]) if upper_static(c, side) else (lists[c] + lists[c ^ mask])
            for c in range(context_size)
        ]
    assert all(entry == lists[0] for entry in lists)
    return lists[0]


def exchange_gather(block, steps, axis_name, count):
    index = lax.axis_index(axis_name)
    stack = block
    for mask, side in steps:
        received = lax.ppermute(stack, axis_name, [(i, i ^ mask) for i in range(count)])
        stack = jnp.where(
            upper_of(index, side),
            jnp.concatenate([received, stack], 1),
            jnp.concatenate([stack, received], 1),
        )
    return stack


def unpermute_blocks(product, sources, x_size):
    rows = product.shape[0]
    count = len(sources)
    y_count = count // x_size
    x_order = [sources[ix * y_count] % x_size for ix in range(x_size)]
    y_order = [sources[iy] // x_size for iy in range(y_count)]
    assert all(
        sources[ix * y_count + iy] == y_order[iy] * x_size + x_order[ix]
        for ix in range(x_size)
        for iy in range(y_count)
    )
    product = product.reshape(rows, x_size, y_count, -1)
    x_inverse = [x_order.index(x) for x in range(x_size)]
    y_inverse = [y_order.index(y) for y in range(y_count)]
    if x_inverse != list(range(x_size)):
        product = jnp.concatenate([product[:, i : i + 1] for i in x_inverse], axis=1)
    if y_inverse != list(range(y_count)):
        product = jnp.concatenate([product[:, :, i : i + 1] for i in y_inverse], axis=2)
    return jnp.swapaxes(product, 1, 2).reshape(rows, -1)


def exchange_gather_pair(stack_a, steps_a, stack_b, steps_b, axis_name, count):
    index = lax.axis_index(axis_name)
    for (mask_a, side_a), (mask_b, side_b) in zip(steps_a, steps_b):
        received_a = lax.ppermute(stack_a, axis_name, [(i, i ^ mask_a) for i in range(count)])
        received_b = lax.ppermute(stack_b, axis_name, [(i, i ^ mask_b) for i in range(count)])
        stack_a = jnp.where(
            upper_of(index, side_a),
            jnp.concatenate([received_a, stack_a], 1),
            jnp.concatenate([stack_a, received_a], 1),
        )
        stack_b = jnp.where(
            upper_of(index, side_b),
            jnp.concatenate([received_b, stack_b], 1),
            jnp.concatenate([stack_b, received_b], 1),
        )
        stack_a, stack_b = lax.optimization_barrier((stack_a, stack_b))
    return stack_a, stack_b


def restack(stack, sources, target, x_size):
    rows, count = stack.shape[:2]
    y_count = count // x_size
    x_from = [sources[ix * y_count] for ix in range(x_size)]
    x_to = [target[ix * y_count] for ix in range(x_size)]
    assert all(
        sources[ix * y_count + iy] - x_from[ix] == target[ix * y_count + iy] - x_to[ix]
        for ix in range(x_size)
        for iy in range(y_count)
    )
    picks = [x_from.index(x) for x in x_to]
    if picks == list(range(x_size)):
        return stack
    stack = stack.reshape(rows, x_size, y_count, -1)
    stack = jnp.concatenate([stack[:, i : i + 1] for i in picks], axis=1)
    return stack.reshape(rows, count, -1)


def per_device(queries, keys, values, order, out_weight):
    row_count = queries.shape[0]
    local_groups = keys.shape[1] // HEAD_SIZE
    query_head_group = QUERY_HEADS // KEY_VALUE_HEADS
    score_scale = 1.0 / math.sqrt(HEAD_SIZE)
    context_size = lax.axis_size("context")
    dp_size = lax.axis_size("dp")
    x_size = X_SIZE if context_size % X_SIZE == 0 and context_size > X_SIZE else 1

    core = lax.axis_index("dp") % 2
    weight_rows, weight_cols = out_weight.shape
    half_rows = weight_rows // 2
    quarter = half_rows // 2
    mine = lax.dynamic_slice_in_dim(out_weight, core * half_rows, half_rows, 0)
    steps_a = chain_plan(context_size, x_size, 1)
    steps_b = chain_plan(context_size, x_size, 3)
    shared = 0
    while shared < min(len(steps_a), len(steps_b)) and steps_a[shared] == steps_b[shared]:
        shared += 1
    key_width = keys.shape[1]
    quarters = [
        mine[k * quarter : (k + 1) * quarter].T.reshape(row_count, -1) for k in range(2)
    ]
    block = jnp.concatenate([keys, quarters[0], values, quarters[1]], axis=1)[:, None, :]
    gathered = exchange_gather(block, steps_a[:shared], "context", context_size)
    gathered_a, gathered_b = exchange_gather_pair(
        gathered[:, :, : key_width + weight_cols],
        steps_a[shared:],
        gathered[:, :, key_width + weight_cols :],
        steps_b[shared:],
        "context",
        context_size,
    )
    sources_a = stacked_sources(context_size, steps_a)
    sources_b = stacked_sources(context_size, steps_b)

    mine_weights = jnp.concatenate(
        [gathered_a[:, :, key_width:], gathered_b[:, :, values.shape[1] :]], axis=0
    )
    other_weights = lax.ppermute(mine_weights, "dp", [(i, i ^ 1) for i in range(dp_size)])

    whole_rows = local_groups == 1
    key_stack = gathered_a if whole_rows else gathered_a[:, :, :key_width]
    value_stack = restack(gathered_b[:, :, : values.shape[1]], sources_b, sources_a, x_size)
    key_part = jnp.swapaxes(key_stack, 0, 1).reshape(context_size * row_count, -1)
    value_part = jnp.swapaxes(value_stack, 0, 1).reshape(context_size * row_count, -1)
    key_pos = order.reshape(context_size, row_count)[jnp.array(sources_a)].reshape(-1)

    first_row = lax.axis_index("context") * row_count
    query_pos = lax.dynamic_slice_in_dim(order, first_row, row_count, 0)
    stacked = queries.reshape(row_count, local_groups, query_head_group, HEAD_SIZE)
    stacked = stacked.transpose(1, 2, 0, 3).reshape(
        local_groups, query_head_group * row_count, HEAD_SIZE
    )
    stacked_pos = jnp.tile(query_pos, query_head_group)
    stacked_rows = query_head_group * row_count
    key_count = key_part.shape[0]
    running_max = jnp.full((local_groups, stacked_rows), -1e30, jnp.float32)
    key_heads = key_part.reshape(key_count, local_groups, -1)
    if whole_rows:
        stacked = jnp.pad(stacked, ((0, 0), (0, 0), (0, key_heads.shape[2] - HEAD_SIZE)))
    value_heads = value_part.reshape(key_count, local_groups, HEAD_SIZE)
    scores = (
        jnp.einsum("grd,kgd->grk", stacked, key_heads, preferred_element_type=jnp.float32)
        * score_scale
    )
    visible = key_pos[None, None, :] <= stacked_pos[None, :, None]
    scores = jnp.where(visible, scores, -1e30)
    new_max = jnp.maximum(running_max, jnp.max(scores, axis=2))
    weights = jnp.where(visible, jnp.exp(scores - new_max[..., None]), 0.0)
    new_sum = jnp.sum(weights, axis=2)
    if whole_rows and x_size > 1:
        y_count = context_size // x_size
        group = y_count * row_count
        x_a = [sources_a[ix * y_count] for ix in range(x_size)]
        x_b = [sources_b[ix * y_count] for ix in range(x_size)]
        value_rows = jnp.swapaxes(gathered_b, 0, 1).reshape(context_size * row_count, -1)
        probs = weights.astype(jnp.bfloat16)
        product = None
        for ia, x in enumerate(x_a):
            ib = x_b.index(x)
            part = jnp.einsum(
                "grk,kd->grd",
                probs[:, :, ia * group : (ia + 1) * group],
                value_rows[ib * group : (ib + 1) * group],
                preferred_element_type=jnp.float32,
            )
            product = part if product is None else product + part
        product = product[:, :, :HEAD_SIZE]
    else:
        product = jnp.einsum(
            "grk,kgd->grd",
            weights.astype(jnp.bfloat16),
            value_heads,
            preferred_element_type=jnp.float32,
        )
    attended = (product / new_sum[..., None]).astype(jnp.bfloat16)
    attended = attended.reshape(local_groups, query_head_group, row_count, HEAD_SIZE).transpose(
        2, 0, 1, 3
    )
    attended = attended.reshape(row_count, local_groups * query_head_group * HEAD_SIZE)

    total = None
    for piece, sources in ((0, sources_a), (1, sources_b)):
        for which, held in ((0, mine_weights), (1, other_weights)):
            piece_t = held[piece * row_count : (piece + 1) * row_count]
            piece_t = jnp.swapaxes(piece_t, 0, 1).reshape(context_size, weight_cols, quarter)
            owner = core if which == 0 else 1 - core
            piece_rows = lax.dynamic_slice_in_dim(
                attended, owner * half_rows + piece * quarter, quarter, 1
            )
            product_out = jnp.einsum(
                "rh,nkh->rnk", piece_rows, piece_t, preferred_element_type=jnp.float32
            ).reshape(row_count, -1)
            product_out = unpermute_blocks(product_out, sources, x_size)
            total = product_out if total is None else total + product_out
    partial_out = total
    tensor_size = lax.axis_size("tensor")
    pieces = partial_out.astype(jnp.bfloat16).reshape(row_count, tensor_size, -1)
    pieces = lax.all_to_all(pieces, "tensor", 1, 1, tiled=True)
    return jnp.sum(pieces.astype(jnp.float32), axis=1).astype(jnp.bfloat16)


def solution(mesh):
    placed = (
        P(("dp", "context"), "tensor"),
        P(("dp", "context"), "tensor"),
        P(("dp", "context"), "tensor"),
        P("dp"),
        P("tensor", "context"),
    )
    return jax.shard_map(
        per_device,
        mesh=mesh,
        in_specs=placed,
        out_specs=P(("dp", "context"), "tensor"),
        check_vma=False,
    )
```

```python
import math

import jax
import jax.numpy as jnp
from jax import lax
from jax.sharding import PartitionSpec as P

QUERY_HEADS = 32
KEY_VALUE_HEADS = 8
HEAD_SIZE = 128
X_SIZE = 4


def chain_plan(context_size, x_size, x_first_mask):
    y_bits = [x_size << k for k in range((context_size // x_size).bit_length() - 1)][::-1]
    steps = [(bit, bit) for bit in y_bits]
    if x_size == 4:
        steps += [(1, 1), (3, 2)] if x_first_mask == 1 else [(3, 2), (1, 3)]
    else:
        steps += [(1 << k, 1 << k) for k in range(x_size.bit_length() - 1)]
    return steps


def upper_of(index, mask):
    bits = index & mask
    parity = jnp.zeros_like(index)
    for k in range(mask.bit_length()):
        parity = parity ^ ((bits >> k) & 1)
    return parity != 0


def upper_static(index, mask):
    return bin(index & mask).count("1") % 2 == 1


def stacked_sources(context_size, steps):
    lists = [[c] for c in range(context_size)]
    for mask, side in steps:
        lists = [
            (lists[c ^ mask] + lists[c]) if upper_static(c, side) else (lists[c] + lists[c ^ mask])
            for c in range(context_size)
        ]
    assert all(entry == lists[0] for entry in lists)
    return lists[0]


def exchange_gather(block, steps, axis_name, count):
    index = lax.axis_index(axis_name)
    stack = block
    for mask, side in steps:
        received = lax.ppermute(stack, axis_name, [(i, i ^ mask) for i in range(count)])
        stack = jnp.where(
            upper_of(index, side),
            jnp.concatenate([received, stack], 1),
            jnp.concatenate([stack, received], 1),
        )
    return stack


def unpermute_blocks(product, sources, x_size):
    rows = product.shape[0]
    count = len(sources)
    y_count = count // x_size
    x_order = [sources[ix * y_count] % x_size for ix in range(x_size)]
    y_order = [sources[iy] // x_size for iy in range(y_count)]
    assert all(
        sources[ix * y_count + iy] == y_order[iy] * x_size + x_order[ix]
        for ix in range(x_size)
        for iy in range(y_count)
    )
    product = product.reshape(rows, x_size, y_count, -1)
    x_inverse = [x_order.index(x) for x in range(x_size)]
    y_inverse = [y_order.index(y) for y in range(y_count)]
    if x_inverse != list(range(x_size)):
        product = jnp.concatenate([product[:, i : i + 1] for i in x_inverse], axis=1)
    if y_inverse != list(range(y_count)):
        product = jnp.concatenate([product[:, :, i : i + 1] for i in y_inverse], axis=2)
    return jnp.swapaxes(product, 1, 2).reshape(rows, -1)


def exchange_gather_pair(stack_a, steps_a, stack_b, steps_b, axis_name, count):
    index = lax.axis_index(axis_name)
    for (mask_a, side_a), (mask_b, side_b) in zip(steps_a, steps_b):
        received_a = lax.ppermute(stack_a, axis_name, [(i, i ^ mask_a) for i in range(count)])
        received_b = lax.ppermute(stack_b, axis_name, [(i, i ^ mask_b) for i in range(count)])
        stack_a = jnp.where(
            upper_of(index, side_a),
            jnp.concatenate([received_a, stack_a], 1),
            jnp.concatenate([stack_a, received_a], 1),
        )
        stack_b = jnp.where(
            upper_of(index, side_b),
            jnp.concatenate([received_b, stack_b], 1),
            jnp.concatenate([stack_b, received_b], 1),
        )
        stack_a, stack_b = lax.optimization_barrier((stack_a, stack_b))
    return stack_a, stack_b


def restack(stack, sources, target, x_size):
    rows, count = stack.shape[:2]
    y_count = count // x_size
    x_from = [sources[ix * y_count] for ix in range(x_size)]
    x_to = [target[ix * y_count] for ix in range(x_size)]
    assert all(
        sources[ix * y_count + iy] - x_from[ix] == target[ix * y_count + iy] - x_to[ix]
        for ix in range(x_size)
        for iy in range(y_count)
    )
    picks = [x_from.index(x) for x in x_to]
    if picks == list(range(x_size)):
        return stack
    stack = stack.reshape(rows, x_size, y_count, -1)
    stack = jnp.concatenate([stack[:, i : i + 1] for i in picks], axis=1)
    return stack.reshape(rows, count, -1)


def per_device(queries, keys, values, order, out_weight):
    row_count = queries.shape[0]
    local_groups = keys.shape[1] // HEAD_SIZE
    query_head_group = QUERY_HEADS // KEY_VALUE_HEADS
    score_scale = 1.0 / math.sqrt(HEAD_SIZE)
    context_size = lax.axis_size("context")
    dp_size = lax.axis_size("dp")
    x_size = X_SIZE if context_size % X_SIZE == 0 and context_size > X_SIZE else 1

    core = lax.axis_index("dp") % 2
    weight_rows, weight_cols = out_weight.shape
    half_rows = weight_rows // 2
    quarter = half_rows // 2
    mine = lax.dynamic_slice_in_dim(out_weight, core * half_rows, half_rows, 0)
    steps_a = chain_plan(context_size, x_size, 1)
    steps_b = chain_plan(context_size, x_size, 3)
    shared = 0
    while shared < min(len(steps_a), len(steps_b)) and steps_a[shared] == steps_b[shared]:
        shared += 1
    key_width = keys.shape[1]
    quarters = [
        mine[k * quarter : (k + 1) * quarter].T.reshape(row_count, -1) for k in range(2)
    ]
    block = jnp.concatenate([keys, quarters[0], values, quarters[1]], axis=1)[:, None, :]
    gathered = exchange_gather(block, steps_a[:shared], "context", context_size)
    gathered_a, gathered_b = exchange_gather_pair(
        gathered[:, :, : key_width + weight_cols],
        steps_a[shared:],
        gathered[:, :, key_width + weight_cols :],
        steps_b[shared:],
        "context",
        context_size,
    )
    sources_a = stacked_sources(context_size, steps_a)
    sources_b = stacked_sources(context_size, steps_b)

    other_a, other_b = lax.ppermute(
        (gathered_a, gathered_b), "dp", [(i, i ^ 1) for i in range(dp_size)]
    )
    mine_weights = (gathered_a[:, :, key_width:], gathered_b[:, :, values.shape[1] :])
    other_weights = (other_a[:, :, key_width:], other_b[:, :, values.shape[1] :])

    whole_rows = local_groups == 1
    key_stack = gathered_a if whole_rows else gathered_a[:, :, :key_width]
    value_stack = restack(gathered_b[:, :, : values.shape[1]], sources_b, sources_a, x_size)
    key_part = jnp.swapaxes(key_stack, 0, 1).reshape(context_size * row_count, -1)
    value_part = jnp.swapaxes(value_stack, 0, 1).reshape(context_size * row_count, -1)
    key_pos = order.reshape(context_size, row_count)[jnp.array(sources_a)].reshape(-1)

    first_row = lax.axis_index("context") * row_count
    query_pos = lax.dynamic_slice_in_dim(order, first_row, row_count, 0)
    stacked = queries.reshape(row_count, local_groups, query_head_group, HEAD_SIZE)
    stacked = stacked.transpose(1, 2, 0, 3).reshape(
        local_groups, query_head_group * row_count, HEAD_SIZE
    )
    stacked_pos = jnp.tile(query_pos, query_head_group)
    stacked_rows = query_head_group * row_count
    key_count = key_part.shape[0]
    running_max = jnp.full((local_groups, stacked_rows), -1e30, jnp.float32)
    key_heads = key_part.reshape(key_count, local_groups, -1)
    if whole_rows:
        stacked = jnp.pad(stacked, ((0, 0), (0, 0), (0, key_heads.shape[2] - HEAD_SIZE)))
    value_heads = value_part.reshape(key_count, local_groups, HEAD_SIZE)
    scores = (
        jnp.einsum("grd,kgd->grk", stacked, key_heads, preferred_element_type=jnp.float32)
        * score_scale
    )
    visible = key_pos[None, None, :] <= stacked_pos[None, :, None]
    scores = jnp.where(visible, scores, -1e30)
    new_max = jnp.maximum(running_max, jnp.max(scores, axis=2))
    weights = jnp.where(visible, jnp.exp(scores - new_max[..., None]), 0.0)
    new_sum = jnp.sum(weights, axis=2)
    product = jnp.einsum(
        "grk,kgd->grd",
        weights.astype(jnp.bfloat16),
        value_heads,
        preferred_element_type=jnp.float32,
    )
    attended = (product / new_sum[..., None]).astype(jnp.bfloat16)
    attended = attended.reshape(local_groups, query_head_group, row_count, HEAD_SIZE).transpose(
        2, 0, 1, 3
    )
    attended = attended.reshape(row_count, local_groups * query_head_group * HEAD_SIZE)

    total = None
    for piece, sources in ((0, sources_a), (1, sources_b)):
        for which, held in ((0, mine_weights), (1, other_weights)):
            piece_t = held[piece]
            piece_t = jnp.swapaxes(piece_t, 0, 1).reshape(context_size, weight_cols, quarter)
            owner = core if which == 0 else 1 - core
            piece_rows = lax.dynamic_slice_in_dim(
                attended, owner * half_rows + piece * quarter, quarter, 1
            )
            product_out = jnp.einsum(
                "rh,nkh->rnk", piece_rows, piece_t, preferred_element_type=jnp.float32
            ).reshape(row_count, -1)
            product_out = unpermute_blocks(product_out, sources, x_size)
            total = product_out if total is None else total + product_out
    partial_out = total
    tensor_size = lax.axis_size("tensor")
    pieces = partial_out.astype(jnp.bfloat16).reshape(row_count, tensor_size, -1)
    pieces = lax.all_to_all(pieces, "tensor", 1, 1, tiled=True)
    return jnp.sum(pieces.astype(jnp.float32), axis=1).astype(jnp.bfloat16)


def solution(mesh):
    placed = (
        P(("dp", "context"), "tensor"),
        P(("dp", "context"), "tensor"),
        P(("dp", "context"), "tensor"),
        P("dp"),
        P("tensor", "context"),
    )
    return jax.shard_map(
        per_device,
        mesh=mesh,
        in_specs=placed,
        out_specs=P(("dp", "context"), "tensor"),
        check_vma=False,
    )
```
